256 devices in a mesh: px: 8 (over y, core), py: 32 (over z, x).
Axes of the slice: x: 4, y: 4, z: 8, core: 2. Of those that a mesh axis runs over, the one named last changes fastest.
Arguments:
- gamma: float32 [256, 256, 256], P('px', 'py'), may hold values from -10 to 10
- positions: float32 [3, 262144], P(None, ('px', 'py')), may hold values from 0 to 16
- weights: float32 [262144], P(('px', 'py')), may hold values from -4 to 4
- block_order: int32 [256, 1024], P(('px', 'py')), may hold values from 0 to 1023, each once within a row
- cell_index: int32 [262144], P(('px', 'py')), may hold values from 0 to 65535
- pair_dest: int32 [65536, 1], P(('px', 'py')), may hold values from 0 to 255; in each aligned block of 256 rows (0 to 255, 256 to 511, ...) at most 2 rows name the same one
- pair_blocks: int32 [2, 65536], P(None, ('px', 'py')), may hold values from 0 to 7
Outputs:
- stress: float32 [256, 256, 256], P('px', 'py')
- glide_force: float32 [262144], P(('px', 'py'))
- new_gamma: float32 [256, 256, 256], P('px', 'py')
The draws below stay inside these ranges and needn't reach their ends.
Inputs may be any that keep to these rules, and one draw needn't show every extreme that they name: `pair_dest`: among the pairs of one device, at most 2 name the same destination device, a bound that some block reaches of them. `block_order`: each row is a permutation of the device's 1024 segments.
All inputs are finite; a program needn't handle non-finite values.
Results may differ from the reference program's by a relative error of at most 0.0003.
Values sent between devices are 32-bit elements; how exact they have to be, the bound alone decides.
No kernel may reach another device: no remote copies, remote signals or barrier semaphores. Data moves between devices by JAX's collectives and lax.ppermute only.
A program may use at most 64 MiB of HBM per device.

```python
import math
import jax
import jax.numpy as jnp
import numpy as np
from jax import lax

G = 256
BLK = 128
BLOCKS_DEV = 8
PAIRS_DEV = 256
SEG_DEV = 1024
SEGS = 262144
PAIRS = 65536
CAP = 2
CELLS_DEV = 65536
N_PX = 8
N_PY = 32
DEVICES = 256


def draw_gamma(key, part):
    jagged = jnp.clip(jax.random.normal(key, (G, G, G), jnp.float32), -5.0, 5.0)
    return jagged


def touch_ends(result, key, low, largest):
    longest = result.shape.index(max(result.shape))
    spots = []
    for shift in (0, 1):
        where = [jax.random.randint(jax.random.fold_in(key, axis), (), 0, length) for axis, length in enumerate(result.shape)]
        where[longest] = (where[longest] + shift) % result.shape[longest]
        spots.append(tuple(where))
    return result.at[spots[0]].set(low).at[spots[1]].set(largest)


def steps_of(rng, shape, pieces, low, top_value):
    level = 1.0
    for axis_at, blocks in pieces:
        heights = jax.random.uniform(jax.random.fold_in(jax.random.fold_in(rng, 6), axis_at), (blocks,), jnp.float32, low / len(pieces), top_value / len(pieces))
        level = level * jnp.repeat(jnp.exp(heights), shape[axis_at] // blocks).reshape((-1,) + (1,) * (len(shape) - 1 - axis_at))
    return level


def routed_block(own_key, own, number, rows, amount, top, limit, skew):
    order = jax.random.permutation(own_key, amount)
    heavy_load, usual = shares(amount, rows * top, limit, skew, True), shares(amount, rows * top, limit, skew, False)
    places = jnp.arange(amount)

    def named(lengths, turn):
        used = int((lengths > 0).sum())
        fixed = max(1, used // 4)
        moved = fixed + (places - fixed + turn * (used - fixed)) % max(1, amount - fixed)
        return jnp.zeros((amount,), jnp.int32).at[order[jnp.where(places < fixed, places, moved)]].set(jnp.asarray(lengths, jnp.int32))

    lengths = jnp.where(number % 4 == 0, named(heavy_load, number // 4), named(usual, number - number // 4 - 1))
    mixed = jax.random.permutation(jax.random.fold_in(own, 3), amount)
    source_of, taker = mixed[0:amount // 2 * 2:2], mixed[1:amount // 2 * 2:2]
    room = jnp.minimum(lengths[source_of] - 1, limit - lengths[taker]) // 2
    room = jnp.where((source_of == order[0]) | (taker == order[0]) | (lengths[taker] == 0), 0, jnp.maximum(room, 0))
    moved = jax.random.randint(jax.random.fold_in(own, 4), (amount // 2,), 0, 1 << 20) % (room + 1)
    lengths = lengths.at[source_of].add(-moved).at[taker].add(moved)
    labels = jnp.searchsorted(jnp.cumsum(lengths), jnp.arange(rows * top), side="right").astype(jnp.int32)
    table = labels.reshape(top, rows).T
    table = table[jax.random.permutation(jax.random.fold_in(own, 1), rows)]
    turn = jax.random.randint(jax.random.fold_in(own, 2), (rows, 1), 0, top)
    return jnp.take_along_axis(table, (jnp.arange(top)[None, :] + turn) % top, axis=1)


def shares(number_of, total, reach, lean, full):
    weights = [(1 << 20) // math.isqrt(grade ** lean) + 1 for grade in range(1, number_of + 1)]
    largest = reach if full else min(reach, max(-(-total // number_of), total * weights[0] // sum(weights)))
    least = 1 if total - largest >= number_of - 1 else 0
    given, surplus = [largest] + [least] * (number_of - 1), total - largest - least * (number_of - 1)
    while surplus > 0:
        movable = [i for i in range(1, number_of) if given[i] < largest] or [i for i in range(1, number_of) if given[i] < reach]
        pool, left = sum([weights[i] for i in movable]), surplus
        for i in movable:
            addition = min(reach - given[i], max(1, left * weights[i] // pool), surplus)
            given[i] = given[i] + addition
            surplus = surplus - addition
    return np.array(given)


def scatter_about(stream_key, dims, scale, bound, shards=(), kind=jnp.bfloat16):
    loudness = steps_of(stream_key, dims, shards, -0.22, 0.18) if shards else 1.0
    result = jax.random.normal(stream_key, dims, jnp.float32) * scale * loudness
    return jnp.minimum(jnp.maximum(result, -bound), bound).astype(kind)


def setup_inputs(seed: int = 0) -> dict:
    keys = jax.random.split(jax.random.key(seed), 8)
    gamma = draw_gamma(jax.random.fold_in(keys[7], 71), 0)
    positions = jnp.clip(16.0 * jax.random.uniform(keys[1], (3, SEGS), jnp.float32) ** steps_of(keys[1], (3, SEGS), ((1, 256),), -0.2, 0.2), 0.0, 16.0)
    weights = scatter_about(keys[2], (SEGS,), 1.0, 4.0, ((0, 256),), jnp.float32)
    block_order = jax.vmap(lambda own: jax.random.permutation(own, SEG_DEV))(jax.random.split(keys[3], DEVICES)).reshape((DEVICES, SEG_DEV)).astype(jnp.int32)
    cell_index = touch_ends(jax.random.randint(keys[4], (SEGS,), 0, CELLS_DEV), jax.random.fold_in(keys[4], 1), 0, CELLS_DEV - 1).astype(jnp.int32)
    pair_dest_keys = jax.random.split(jax.random.fold_in(keys[5], 1), PAIRS // PAIRS_DEV)
    pair_dest_turns = jax.random.permutation(jax.random.fold_in(keys[5], 3), PAIRS // PAIRS_DEV)
    pair_dest = jax.vmap(lambda own, number: routed_block(jax.random.fold_in(keys[5], 2), own, number, PAIRS_DEV, DEVICES, 1, CAP, 2))(pair_dest_keys, pair_dest_turns).reshape((PAIRS, 1))
    pair_blocks = touch_ends(jax.random.randint(keys[6], (2, PAIRS), 0, BLOCKS_DEV), jax.random.fold_in(keys[6], 1), 0, BLOCKS_DEV - 1).astype(jnp.int32)
    return dict(gamma=gamma, positions=positions, weights=weights, block_order=block_order, cell_index=cell_index, pair_dest=pair_dest, pair_blocks=pair_blocks)


POISSON = 0.34
STEP_MOBILITY = 0.5
CORE_SQUARED = 1.0
ROOT_HALF = 0.7071067811865476

def wrapped(indices, number):
    shifted = jnp.where(indices == number // 2, 0, indices - number)
    return jnp.where(indices < number // 2, indices, shifted).astype(jnp.float32)

def multiplier(first, second, third):
    summed = first * first + second * second + third * third
    bounded = jnp.maximum(summed, 1.0)
    normal_part = (first + second + third) ** 2 / (3.0 * bounded)
    slip_part = (first - second) ** 2 / (2.0 * bounded)
    factor = normal_part + slip_part - 2.0 * normal_part * slip_part / (1.0 - POISSON) - 1.0
    return jnp.where(summed > 0.5, factor, 0.0)

def pair_terms(target, source):
    offset = target[:, 0:3, :, None] - source[:, 0:3, None, :]
    squared = offset[:, 0] * offset[:, 0] + offset[:, 1] * offset[:, 1] + offset[:, 2] * offset[:, 2] + CORE_SQUARED
    along = (offset[:, 0] - offset[:, 1]) * ROOT_HALF
    strength = target[:, 3, :, None] * source[:, 3, None, :]
    coupling = strength * along / (squared * jnp.sqrt(squared))
    return (lax.optimization_barrier(jnp.sum(coupling, axis=2)), -lax.optimization_barrier(jnp.sum(coupling, axis=1)))

def reference(gamma, positions, weights, block_order, cell_index, pair_dest, pair_blocks):
    seg_dev = BLOCKS_DEV * BLK
    devices = N_PX * N_PY
    members = (block_order + seg_dev * jnp.arange(devices, dtype=jnp.int32)[:, None]).reshape(devices * BLOCKS_DEV, BLK)
    payload = jnp.concatenate([positions, weights[None, :]], 0)
    blocks = jnp.transpose(payload[:, members], (1, 0, 2))
    sender = jnp.arange(PAIRS, dtype=jnp.int32) // PAIRS_DEV
    source_id = sender * BLOCKS_DEV + pair_blocks[0]
    target_id = pair_dest[:, 0] * BLOCKS_DEV + pair_blocks[1]
    grouped = jnp.transpose(jnp.stack([source_id, target_id], 0).reshape(2, PAIRS // 16, 16), (1, 0, 2))

    def one_group(couple):
        return pair_terms(blocks[couple[1]], blocks[couple[0]])
    on_target, on_source = lax.map(one_group, grouped)
    block_force = jnp.zeros((devices * BLOCKS_DEV, BLK), jnp.float32)
    block_force = block_force.at[target_id].add(on_target.reshape(PAIRS, BLK))
    block_force = block_force.at[source_id].add(on_source.reshape(PAIRS, BLK))
    pair_force = jnp.zeros((SEGS,), jnp.float32).at[members.reshape(-1)].set(block_force.reshape(-1))
    freqs = wrapped(jnp.arange(G, dtype=jnp.int32), G)
    factor_table = multiplier(freqs[:, None, None], freqs[None, :, None], freqs[None, None, :])
    stress = jnp.real(jnp.fft.ifftn(jnp.fft.fftn(gamma) * factor_table)).astype(jnp.float32)
    owner = jnp.arange(SEGS, dtype=jnp.int32) // seg_dev
    height = G // N_PX
    breadth = G // N_PY
    first = owner // N_PY * height + cell_index // (breadth * G)
    second = owner % N_PY * breadth + cell_index // G % breadth
    third = cell_index % G
    flat = (first * G + second) * G + third
    glide_force = weights * stress.reshape(-1)[flat] + pair_force
    new_gamma = gamma.reshape(-1).at[flat].add(STEP_MOBILITY * weights * glide_force).reshape(G, G, G)
    return (stress, glide_force, new_gamma)
```

```python
import math

import jax
import jax.numpy as jnp
from jax import lax
from jax.sharding import PartitionSpec as P

BLK = 128


POISSON = 0.34
STEP_MOBILITY = 0.5
CORE_SQUARED = 1.0
ROOT_HALF = 0.7071067811865476


def wrapped(indices, number):
    shifted = jnp.where(indices == number // 2, 0, indices - number)
    return jnp.where(indices < number // 2, indices, shifted).astype(jnp.float32)


def multiplier(first, second, third):
    summed = first * first + second * second + third * third
    bounded = jnp.maximum(summed, 1.0)
    normal_part = (first + second + third) ** 2 / (3.0 * bounded)
    slip_part = (first - second) ** 2 / (2.0 * bounded)
    factor = normal_part + slip_part - 2.0 * normal_part * slip_part / (1.0 - POISSON) - 1.0
    return jnp.where(summed > 0.5, factor, 0.0)


def pair_terms(target, source):
    offset = target[:, 0:3, :, None] - source[:, 0:3, None, :]
    squared = (
        offset[:, 0] * offset[:, 0]
        + offset[:, 1] * offset[:, 1]
        + offset[:, 2] * offset[:, 2]
        + CORE_SQUARED
    )
    along = (offset[:, 0] - offset[:, 1]) * ROOT_HALF
    strength = target[:, 3, :, None] * source[:, 3, None, :]
    coupling = strength * along / (squared * jnp.sqrt(squared))
    return (jnp.sum(coupling, axis=2), -jnp.sum(coupling, axis=1))


def evaluate(target, source):
    number = target.shape[0]
    width = target.shape[2]

    def one_group(couple):
        return pair_terms(couple[0], couple[1])

    on_target, on_source = lax.map(
        one_group,
        (target.reshape(number // 16, 16, 4, width), source.reshape(number // 16, 16, 4, width)),
    )
    return (on_target.reshape(number, width), on_source.reshape(number, width))


def dft_tables(number):
    indices = jnp.arange(number, dtype=jnp.int32)
    phases = indices[:, None] * indices[None, :] % number
    angles = phases.astype(jnp.float32) * (2.0 * math.pi / number)
    return (jnp.cos(angles), jnp.sin(angles))


def contract(form, left, right):
    return jnp.einsum(form, left, right, precision=lax.Precision.HIGHEST)


def rotate(form, real_part, imag_part, cosines, sine_table, direction):
    real_out = contract(form, real_part, cosines) + direction * contract(
        form, imag_part, sine_table
    )
    imag_out = contract(form, imag_part, cosines) - direction * contract(
        form, real_part, sine_table
    )
    return (real_out, imag_out)


def across_rows(real_part, imag_part):
    return (
        lax.all_to_all(real_part, "py", split_axis=1, concat_axis=2, tiled=True),
        lax.all_to_all(imag_part, "py", split_axis=1, concat_axis=2, tiled=True),
    )


def across_columns(real_part, imag_part):
    return (
        lax.all_to_all(real_part, "px", split_axis=0, concat_axis=2, tiled=True),
        lax.all_to_all(imag_part, "px", split_axis=0, concat_axis=2, tiled=True),
    )


def shards(gamma, positions, weights, block_order, cell_index, pair_dest, pair_blocks):
    extent = gamma.shape[2]
    cosines, sine_table = dft_tables(extent)
    real_part = contract("abx,xk->akb", gamma, cosines)
    imag_part = -contract("abx,xk->akb", gamma, sine_table)
    real_part, imag_part = across_rows(real_part, imag_part)
    real_part, imag_part = rotate("aky,ym->mka", real_part, imag_part, cosines, sine_table, 1.0)
    real_part, imag_part = across_columns(real_part, imag_part)
    real_part, imag_part = rotate("mkz,zq->mkq", real_part, imag_part, cosines, sine_table, 1.0)
    rows_local = real_part.shape[0]
    cols_local = real_part.shape[1]
    first_index = lax.axis_index("px") * rows_local + jnp.arange(rows_local, dtype=jnp.int32)
    second_index = lax.axis_index("py") * cols_local + jnp.arange(cols_local, dtype=jnp.int32)
    third_index = jnp.arange(extent, dtype=jnp.int32)
    factor_table = multiplier(
        wrapped(third_index, extent)[None, None, :],
        wrapped(first_index, extent)[:, None, None],
        wrapped(second_index, extent)[None, :, None],
    )
    real_part = real_part * factor_table
    imag_part = imag_part * factor_table
    real_part, imag_part = rotate("mkq,qz->zkm", real_part, imag_part, cosines, sine_table, -1.0)
    real_part, imag_part = across_columns(real_part, imag_part)
    real_part, imag_part = rotate("akm,my->ayk", real_part, imag_part, cosines, sine_table, -1.0)
    real_part, imag_part = across_rows(real_part, imag_part)
    stress = (
        contract("abk,kx->abx", real_part, cosines) - contract("abk,kx->abx", imag_part, sine_table)
    ) / float(extent**3)
    seg_count = positions.shape[1]
    members = block_order[0]
    payload = jnp.concatenate([positions, weights[None, :]], 0)
    blocks = jnp.transpose(payload[:, members.reshape(-1, BLK)], (1, 0, 2))
    local_blocks = blocks.shape[0]
    seg_width = blocks.shape[2]
    source_local = pair_blocks[0]
    target_block = pair_blocks[1]
    destination = pair_dest[:, 0]
    pairs = destination.shape[0]
    devices = lax.psum(1, ("px", "py"))
    cap = 2
    earlier = jnp.sum(
        (destination[:, None] == destination[None, :])
        & (jnp.arange(pairs)[:, None] > jnp.arange(pairs)[None, :]),
        axis=1,
        dtype=jnp.int32,
    )
    slot = destination * cap + earlier
    wanted = jnp.zeros((devices * cap,), jnp.int32).at[slot].set(target_block)
    asked = lax.all_to_all(
        wanted.reshape(devices, cap), ("px", "py"), 0, 0, tiled=True
    ).reshape(-1)
    served = blocks[asked].reshape(devices, cap * 4 * seg_width)
    fetched = lax.all_to_all(served, ("px", "py"), 0, 0, tiled=True).reshape(
        devices * cap, 4, seg_width
    )
    on_target, on_source = evaluate(fetched[slot], blocks[source_local])
    returned = jnp.zeros((devices * cap, seg_width), jnp.float32).at[slot].set(on_target)
    arrived = lax.all_to_all(
        returned.reshape(devices, cap * seg_width), ("px", "py"), 0, 0, tiled=True
    ).reshape(devices * cap, seg_width)
    block_force = (
        jnp.zeros((local_blocks, seg_width), jnp.float32)
        .at[asked]
        .add(arrived)
        .at[source_local]
        .add(on_source)
    )
    pair_force = jnp.zeros((seg_count,), jnp.float32).at[members].set(block_force.reshape(-1))
    flat_stress = stress.reshape(-1)
    glide_force = weights * flat_stress[cell_index] + pair_force
    new_gamma = (
        gamma.reshape(-1)
        .at[cell_index]
        .add(STEP_MOBILITY * weights * glide_force)
        .reshape(gamma.shape)
    )
    return (stress, glide_force, new_gamma)


def solution(mesh):
    in_specs = (
        P("px", "py", None),
        P(None, ("px", "py")),
        P(("px", "py")),
        P(("px", "py"), None),
        P(("px", "py")),
        P(("px", "py"), None),
        P(None, ("px", "py")),
    )
    out_specs = (P("px", "py", None), P(("px", "py")), P("px", "py", None))
    return jax.shard_map(shards, mesh=mesh, in_specs=in_specs, out_specs=out_specs, check_vma=False)
```

```python
import math

import jax
import jax.numpy as jnp
from jax import lax
from jax.experimental import pallas as pl
from jax.sharding import PartitionSpec as P

BLK = 128


POISSON = 0.34
STEP_MOBILITY = 0.5
CORE_SQUARED = 1.0
ROOT_HALF = 0.7071067811865476


def wrapped(indices, number):
    shifted = jnp.where(indices == number // 2, 0, indices - number)
    return jnp.where(indices < number // 2, indices, shifted).astype(jnp.float32)


def multiplier(first, second, third):
    summed = first * first + second * second + third * third
    bounded = jnp.maximum(summed, 1.0)
    normal_part = (first + second + third) ** 2 / (3.0 * bounded)
    slip_part = (first - second) ** 2 / (2.0 * bounded)
    factor = normal_part + slip_part - 2.0 * normal_part * slip_part / (1.0 - POISSON) - 1.0
    return jnp.where(summed > 0.5, factor, 0.0)


def pair_terms(target, source):
    offset = target[:, 0:3, :, None] - source[:, 0:3, None, :]
    squared = (
        offset[:, 0] * offset[:, 0]
        + offset[:, 1] * offset[:, 1]
        + offset[:, 2] * offset[:, 2]
        + CORE_SQUARED
    )
    along = (offset[:, 0] - offset[:, 1]) * ROOT_HALF
    strength = target[:, 3, :, None] * source[:, 3, None, :]
    coupling = strength * along / (squared * jnp.sqrt(squared))
    return (jnp.sum(coupling, axis=2), -jnp.sum(coupling, axis=1))


PAIR_STEP = 8


def pair_kernel(target_ref, source_ref, on_target_ref, on_source_ref):
    ones = jnp.ones((8, BLK), jnp.float32)

    def one_pair(p, carry):
        target = target_ref[p]
        source = source_ref[p]
        columns = jnp.transpose(jnp.concatenate([target, target], 0))
        d0 = columns[:, 0:1] - source[0:1, :]
        d1 = columns[:, 1:2] - source[1:2, :]
        d2 = columns[:, 2:3] - source[2:3, :]
        squared = d0 * d0 + d1 * d1 + d2 * d2 + CORE_SQUARED
        along = (d0 - d1) * ROOT_HALF
        strength = columns[:, 3:4] * source[3:4, :]
        coupling = strength * along / (squared * jnp.sqrt(squared))
        row_sums = lax.dot_general(
            ones,
            coupling,
            (((1,), (1,)), ((), ())),
            precision=lax.Precision.HIGHEST,
            preferred_element_type=jnp.float32,
        )
        on_target_ref[pl.ds(p, 1), :] = row_sums[0:1, :]
        on_source_ref[pl.ds(p, 1), :] = -jnp.sum(coupling, axis=0, keepdims=True)
        return carry

    lax.fori_loop(0, PAIR_STEP, one_pair, 0)


def evaluate(target, source):
    number = target.shape[0]
    width = target.shape[2]
    block_in = pl.BlockSpec((PAIR_STEP, 4, width), lambda i: (i, 0, 0))
    block_out = pl.BlockSpec((PAIR_STEP, width), lambda i: (i, 0))
    return pl.pallas_call(
        pair_kernel,
        grid=(number // PAIR_STEP,),
        in_specs=[block_in, block_in],
        out_specs=[block_out, block_out],
        out_shape=[
            jax.ShapeDtypeStruct((number, width), jnp.float32),
            jax.ShapeDtypeStruct((number, width), jnp.float32),
        ],
    )(target, source)


def dft_tables(number):
    indices = jnp.arange(number, dtype=jnp.int32)
    phases = indices[:, None] * indices[None, :] % number
    angles = phases.astype(jnp.float32) * (2.0 * math.pi / number)
    return (jnp.cos(angles), jnp.sin(angles))


def contract(form, left, right):
    return jnp.einsum(form, left, right, precision=lax.Precision.HIGHEST)


def rotate(form, real_part, imag_part, cosines, sine_table, direction):
    real_out = contract(form, real_part, cosines) + direction * contract(
        form, imag_part, sine_table
    )
    imag_out = contract(form, imag_part, cosines) - direction * contract(
        form, real_part, sine_table
    )
    return (real_out, imag_out)


def across_rows(real_part, imag_part):
    return (
        lax.all_to_all(real_part, "py", split_axis=1, concat_axis=2, tiled=True),
        lax.all_to_all(imag_part, "py", split_axis=1, concat_axis=2, tiled=True),
    )


def across_columns(real_part, imag_part):
    return (
        lax.all_to_all(real_part, "px", split_axis=0, concat_axis=2, tiled=True),
        lax.all_to_all(imag_part, "px", split_axis=0, concat_axis=2, tiled=True),
    )


def cplx_table(number, direction):
    cosines, sine_table = dft_tables(number)
    top = jnp.stack([cosines, -direction * sine_table], 1)
    bottom = jnp.stack([direction * sine_table, cosines], 1)
    return jnp.stack([top, bottom], 0)


def shards(gamma, positions, weights, block_order, cell_index, pair_dest, pair_blocks):
    extent = gamma.shape[2]
    cosines, sine_table = dft_tables(extent)
    forward = cplx_table(extent, 1.0)
    inverse = cplx_table(extent, -1.0)
    spec = contract("abx,xck->cakb", gamma, jnp.stack([cosines, -sine_table], 1))
    spec = lax.all_to_all(spec, "py", split_axis=2, concat_axis=3, tiled=True)
    spec = contract("caky,cydm->dmka", spec, forward)
    spec = lax.all_to_all(spec, "px", split_axis=1, concat_axis=3, tiled=True)
    spec = contract("cmkz,czdq->dmkq", spec, forward)
    rows_local = spec.shape[1]
    cols_local = spec.shape[2]
    first_index = lax.axis_index("px") * rows_local + jnp.arange(rows_local, dtype=jnp.int32)
    second_index = lax.axis_index("py") * cols_local + jnp.arange(cols_local, dtype=jnp.int32)
    third_index = jnp.arange(extent, dtype=jnp.int32)
    factor_table = multiplier(
        wrapped(third_index, extent)[None, None, :],
        wrapped(first_index, extent)[:, None, None],
        wrapped(second_index, extent)[None, :, None],
    )
    spec = spec * factor_table[None]
    spec = contract("cmkq,cqdz->dzkm", spec, inverse)
    spec = lax.all_to_all(spec, "px", split_axis=1, concat_axis=3, tiled=True)
    spec = contract("cakm,cmdy->dayk", spec, inverse)
    spec = lax.all_to_all(spec, "py", split_axis=2, concat_axis=3, tiled=True)
    stress = contract("cabk,ckx->abx", spec, jnp.stack([cosines, -sine_table], 0)) / float(
        extent**3
    )
    seg_count = positions.shape[1]
    members = block_order[0]
    payload = jnp.concatenate([positions, weights[None, :]], 0)
    blocks = jnp.transpose(payload[:, members.reshape(-1, BLK)], (1, 0, 2))
    local_blocks = blocks.shape[0]
    seg_width = blocks.shape[2]
    source_local = pair_blocks[0]
    target_block = pair_blocks[1]
    destination = pair_dest[:, 0]
    pairs = destination.shape[0]
    devices = lax.psum(1, ("px", "py"))
    cap = 2
    earlier = jnp.sum(
        (destination[:, None] == destination[None, :])
        & (jnp.arange(pairs)[:, None] > jnp.arange(pairs)[None, :]),
        axis=1,
        dtype=jnp.int32,
    )
    slot = destination * cap + earlier
    wanted = jnp.zeros((devices * cap,), jnp.int32).at[slot].set(target_block)
    asked = lax.all_to_all(
        wanted.reshape(devices, cap), ("px", "py"), 0, 0, tiled=True
    ).reshape(-1)
    served = blocks[asked].reshape(devices, cap * 4 * seg_width)
    fetched = lax.all_to_all(served, ("px", "py"), 0, 0, tiled=True).reshape(
        devices * cap, 4, seg_width
    )
    on_target, on_source = evaluate(fetched[slot], blocks[source_local])
    returned = jnp.zeros((devices * cap, seg_width), jnp.float32).at[slot].set(on_target)
    arrived = lax.all_to_all(
        returned.reshape(devices, cap * seg_width), ("px", "py"), 0, 0, tiled=True
    ).reshape(devices * cap, seg_width)
    block_force = (
        jnp.zeros((local_blocks, seg_width), jnp.float32)
        .at[asked]
        .add(arrived)
        .at[source_local]
        .add(on_source)
    )
    pair_force = jnp.zeros((seg_count,), jnp.float32).at[members].set(block_force.reshape(-1))
    flat_stress = stress.reshape(-1)
    glide_force = weights * flat_stress[cell_index] + pair_force
    new_gamma = (
        gamma.reshape(-1)
        .at[cell_index]
        .add(STEP_MOBILITY * weights * glide_force)
        .reshape(gamma.shape)
    )
    return (stress, glide_force, new_gamma)


def solution(mesh):
    in_specs = (
        P("px", "py", None),
        P(None, ("px", "py")),
        P(("px", "py")),
        P(("px", "py"), None),
        P(("px", "py")),
        P(("px", "py"), None),
        P(None, ("px", "py")),
    )
    out_specs = (P("px", "py", None), P(("px", "py")), P("px", "py", None))
    return jax.shard_map(shards, mesh=mesh, in_specs=in_specs, out_specs=out_specs, check_vma=False)
```

```python
import math

import jax
import jax.numpy as jnp
from jax import lax
from jax.sharding import PartitionSpec as P

BLK = 128


POISSON = 0.34
STEP_MOBILITY = 0.5
CORE_SQUARED = 1.0
ROOT_HALF = 0.7071067811865476


def wrapped(indices, number):
    shifted = jnp.where(indices == number // 2, 0, indices - number)
    return jnp.where(indices < number // 2, indices, shifted).astype(jnp.float32)


def multiplier(first, second, third):
    summed = first * first + second * second + third * third
    bounded = jnp.maximum(summed, 1.0)
    normal_part = (first + second + third) ** 2 / (3.0 * bounded)
    slip_part = (first - second) ** 2 / (2.0 * bounded)
    factor = normal_part + slip_part - 2.0 * normal_part * slip_part / (1.0 - POISSON) - 1.0
    return jnp.where(summed > 0.5, factor, 0.0)


def pair_terms(target, source):
    offset = target[:, 0:3, :, None] - source[:, 0:3, None, :]
    squared = (
        offset[:, 0] * offset[:, 0]
        + offset[:, 1] * offset[:, 1]
        + offset[:, 2] * offset[:, 2]
        + CORE_SQUARED
    )
    along = (offset[:, 0] - offset[:, 1]) * ROOT_HALF
    strength = target[:, 3, :, None] * source[:, 3, None, :]
    coupling = strength * along / (squared * jnp.sqrt(squared))
    return (jnp.sum(coupling, axis=2), -jnp.sum(coupling, axis=1))


def evaluate(target, source):
    number = target.shape[0]
    width = target.shape[2]

    def one_group(couple):
        return pair_terms(couple[0], couple[1])

    on_target, on_source = lax.map(
        one_group,
        (target.reshape(number // 16, 16, 4, width), source.reshape(number // 16, 16, 4, width)),
    )
    return (on_target.reshape(number, width), on_source.reshape(number, width))


def dft_tables(number):
    indices = jnp.arange(number, dtype=jnp.int32)
    phases = indices[:, None] * indices[None, :] % number
    angles = phases.astype(jnp.float32) * (2.0 * math.pi / number)
    return (jnp.cos(angles), jnp.sin(angles))


def contract(form, left, right):
    return jnp.einsum(form, left, right, precision=lax.Precision.HIGHEST)


def rotate(form, real_part, imag_part, cosines, sine_table, direction):
    real_out = contract(form, real_part, cosines) + direction * contract(
        form, imag_part, sine_table
    )
    imag_out = contract(form, imag_part, cosines) - direction * contract(
        form, real_part, sine_table
    )
    return (real_out, imag_out)


def across_rows(real_part, imag_part):
    return (
        lax.all_to_all(real_part, "py", split_axis=1, concat_axis=2, tiled=True),
        lax.all_to_all(imag_part, "py", split_axis=1, concat_axis=2, tiled=True),
    )


def across_columns(real_part, imag_part):
    return (
        lax.all_to_all(real_part, "px", split_axis=0, concat_axis=2, tiled=True),
        lax.all_to_all(imag_part, "px", split_axis=0, concat_axis=2, tiled=True),
    )


def cplx_table(number, direction):
    cosines, sine_table = dft_tables(number)
    top = jnp.stack([cosines, -direction * sine_table], 1)
    bottom = jnp.stack([direction * sine_table, cosines], 1)
    return jnp.stack([top, bottom], 0)


def shards(gamma, positions, weights, block_order, cell_index, pair_dest, pair_blocks):
    extent = gamma.shape[2]
    cosines, sine_table = dft_tables(extent)
    forward = cplx_table(extent, 1.0)
    inverse = cplx_table(extent, -1.0)
    spec = contract("abx,xck->cakb", gamma, jnp.stack([cosines, -sine_table], 1))
    spec = lax.all_to_all(spec, "py", split_axis=2, concat_axis=3, tiled=True)
    spec = contract("caky,cydm->dmka", spec, forward)
    spec = lax.all_to_all(spec, "px", split_axis=1, concat_axis=3, tiled=True)
    spec = contract("cmkz,czdq->dmkq", spec, forward)
    rows_local = spec.shape[1]
    cols_local = spec.shape[2]
    first_index = lax.axis_index("px") * rows_local + jnp.arange(rows_local, dtype=jnp.int32)
    second_index = lax.axis_index("py") * cols_local + jnp.arange(cols_local, dtype=jnp.int32)
    third_index = jnp.arange(extent, dtype=jnp.int32)
    factor_table = multiplier(
        wrapped(third_index, extent)[None, None, :],
        wrapped(first_index, extent)[:, None, None],
        wrapped(second_index, extent)[None, :, None],
    )
    spec = spec * factor_table[None]
    spec = contract("cmkq,cqdz->dzkm", spec, inverse)
    spec = lax.all_to_all(spec, "px", split_axis=1, concat_axis=3, tiled=True)
    spec = contract("cakm,cmdy->dayk", spec, inverse)
    spec = lax.all_to_all(spec, "py", split_axis=2, concat_axis=3, tiled=True)
    stress = contract("cabk,ckx->abx", spec, jnp.stack([cosines, -sine_table], 0)) / float(
        extent**3
    )
    seg_count = positions.shape[1]
    members = block_order[0]
    payload = jnp.concatenate([positions, weights[None, :]], 0)
    blocks = jnp.transpose(payload[:, members.reshape(-1, BLK)], (1, 0, 2))
    local_blocks = blocks.shape[0]
    seg_width = blocks.shape[2]
    source_local = pair_blocks[0]
    target_block = pair_blocks[1]
    destination = pair_dest[:, 0]
    pairs = destination.shape[0]
    devices = lax.psum(1, ("px", "py"))
    cap = 2
    earlier = jnp.sum(
        (destination[:, None] == destination[None, :])
        & (jnp.arange(pairs)[:, None] > jnp.arange(pairs)[None, :]),
        axis=1,
        dtype=jnp.int32,
    )
    slot = destination * cap + earlier
    wanted = jnp.zeros((devices * cap,), jnp.int32).at[slot].set(target_block)
    asked = lax.all_to_all(
        wanted.reshape(devices, cap), ("px", "py"), 0, 0, tiled=True
    ).reshape(-1)
    served = blocks[asked].reshape(devices, cap * 4 * seg_width)
    fetched = lax.all_to_all(served, ("px", "py"), 0, 0, tiled=True).reshape(
        devices * cap, 4, seg_width
    )
    on_target, on_source = evaluate(fetched[slot], blocks[source_local])
    returned = jnp.zeros((devices * cap, seg_width), jnp.float32).at[slot].set(on_target)
    arrived = lax.all_to_all(
        returned.reshape(devices, cap * seg_width), ("px", "py"), 0, 0, tiled=True
    ).reshape(devices * cap, seg_width)
    block_force = (
        jnp.zeros((local_blocks, seg_width), jnp.float32)
        .at[asked]
        .add(arrived)
        .at[source_local]
        .add(on_source)
    )
    pair_force = jnp.zeros((seg_count,), jnp.float32).at[members].set(block_force.reshape(-1))
    flat_stress = stress.reshape(-1)
    glide_force = weights * flat_stress[cell_index] + pair_force
    new_gamma = (
        gamma.reshape(-1)
        .at[cell_index]
        .add(STEP_MOBILITY * weights * glide_force)
        .reshape(gamma.shape)
    )
    return (stress, glide_force, new_gamma)


def solution(mesh):
    in_specs = (
        P("px", "py", None),
        P(None, ("px", "py")),
        P(("px", "py")),
        P(("px", "py"), None),
        P(("px", "py")),
        P(("px", "py"), None),
        P(None, ("px", "py")),
    )
    out_specs = (P("px", "py", None), P(("px", "py")), P("px", "py", None))
    return jax.shard_map(shards, mesh=mesh, in_specs=in_specs, out_specs=out_specs, check_vma=False)
```

```python
import math

import jax
import jax.numpy as jnp
from jax import lax
from jax.experimental import pallas as pl
from jax.sharding import PartitionSpec as P

BLK = 128


POISSON = 0.34
STEP_MOBILITY = 0.5
CORE_SQUARED = 1.0
ROOT_HALF = 0.7071067811865476


def wrapped(indices, number):
    shifted = jnp.where(indices == number // 2, 0, indices - number)
    return jnp.where(indices < number // 2, indices, shifted).astype(jnp.float32)


def multiplier(first, second, third):
    summed = first * first + second * second + third * third
    bounded = jnp.maximum(summed, 1.0)
    normal_part = (first + second + third) ** 2 / (3.0 * bounded)
    slip_part = (first - second) ** 2 / (2.0 * bounded)
    factor = normal_part + slip_part - 2.0 * normal_part * slip_part / (1.0 - POISSON) - 1.0
    return jnp.where(summed > 0.5, factor, 0.0)


def pair_terms(target, source):
    offset = target[:, 0:3, :, None] - source[:, 0:3, None, :]
    squared = (
        offset[:, 0] * offset[:, 0]
        + offset[:, 1] * offset[:, 1]
        + offset[:, 2] * offset[:, 2]
        + CORE_SQUARED
    )
    along = (offset[:, 0] - offset[:, 1]) * ROOT_HALF
    strength = target[:, 3, :, None] * source[:, 3, None, :]
    coupling = strength * along / (squared * jnp.sqrt(squared))
    return (jnp.sum(coupling, axis=2), -jnp.sum(coupling, axis=1))


PAIR_STEP = 32


def pair_kernel(target_ref, source_ref, on_target_ref, on_source_ref):
    columns = jnp.transpose(target_ref[...].reshape(PAIR_STEP * 4, BLK))
    source_rows = []
    target_rows = []
    for p in range(PAIR_STEP):
        source = source_ref[p]
        d0 = columns[:, 4 * p : 4 * p + 1] - source[0:1, :]
        d1 = columns[:, 4 * p + 1 : 4 * p + 2] - source[1:2, :]
        d2 = columns[:, 4 * p + 2 : 4 * p + 3] - source[2:3, :]
        squared = d0 * d0 + d1 * d1 + d2 * d2 + CORE_SQUARED
        along = (d0 - d1) * ROOT_HALF
        strength = columns[:, 4 * p + 3 : 4 * p + 4] * source[3:4, :]
        root = lax.rsqrt(squared)
        coupling = strength * along * (root * root * root)
        source_rows.append(-jnp.sum(coupling, axis=0, keepdims=True))
        target_rows.append(jnp.sum(jnp.transpose(coupling), axis=0, keepdims=True))
    on_source_ref[...] = jnp.concatenate(source_rows, 0)
    on_target_ref[...] = jnp.concatenate(target_rows, 0)


def evaluate(target, source):
    number = target.shape[0]
    width = target.shape[2]
    block_in = pl.BlockSpec((PAIR_STEP, 4, width), lambda i: (i, 0, 0))
    block_out = pl.BlockSpec((PAIR_STEP, width), lambda i: (i, 0))
    return pl.pallas_call(
        pair_kernel,
        grid=(number // PAIR_STEP,),
        in_specs=[block_in, block_in],
        out_specs=[block_out, block_out],
        out_shape=[jax.ShapeDtypeStruct((number, width), jnp.float32)] * 2,
    )(target, source)


def dft_tables(number):
    indices = jnp.arange(number, dtype=jnp.int32)
    phases = indices[:, None] * indices[None, :] % number
    angles = phases.astype(jnp.float32) * (2.0 * math.pi / number)
    return (jnp.cos(angles), jnp.sin(angles))


def contract(form, left, right):
    return jnp.einsum(form, left, right, precision=lax.Precision.HIGHEST)


def rotate(form, real_part, imag_part, cosines, sine_table, direction):
    real_out = contract(form, real_part, cosines) + direction * contract(
        form, imag_part, sine_table
    )
    imag_out = contract(form, imag_part, cosines) - direction * contract(
        form, real_part, sine_table
    )
    return (real_out, imag_out)


def across_rows(real_part, imag_part):
    return (
        lax.all_to_all(real_part, "py", split_axis=1, concat_axis=2, tiled=True),
        lax.all_to_all(imag_part, "py", split_axis=1, concat_axis=2, tiled=True),
    )


def across_columns(real_part, imag_part):
    return (
        lax.all_to_all(real_part, "px", split_axis=0, concat_axis=2, tiled=True),
        lax.all_to_all(imag_part, "px", split_axis=0, concat_axis=2, tiled=True),
    )


def cplx_table(number, direction):
    cosines, sine_table = dft_tables(number)
    top = jnp.stack([cosines, -direction * sine_table], 1)
    bottom = jnp.stack([direction * sine_table, cosines], 1)
    return jnp.stack([top, bottom], 0)


def shards(gamma, positions, weights, block_order, cell_index, pair_dest, pair_blocks):
    extent = gamma.shape[2]
    cosines, sine_table = dft_tables(extent)
    forward = cplx_table(extent, 1.0)
    inverse = cplx_table(extent, -1.0)
    spec = contract("abx,xck->cakb", gamma, jnp.stack([cosines, -sine_table], 1))
    spec = lax.all_to_all(spec, "py", split_axis=2, concat_axis=3, tiled=True)
    spec = contract("caky,cydm->dmka", spec, forward)
    spec = lax.all_to_all(spec, "px", split_axis=1, concat_axis=3, tiled=True)
    spec = contract("cmkz,czdq->dmkq", spec, forward)
    rows_local = spec.shape[1]
    cols_local = spec.shape[2]
    first_index = lax.axis_index("px") * rows_local + jnp.arange(rows_local, dtype=jnp.int32)
    second_index = lax.axis_index("py") * cols_local + jnp.arange(cols_local, dtype=jnp.int32)
    third_index = jnp.arange(extent, dtype=jnp.int32)
    factor_table = multiplier(
        wrapped(third_index, extent)[None, None, :],
        wrapped(first_index, extent)[:, None, None],
        wrapped(second_index, extent)[None, :, None],
    )
    spec = spec * factor_table[None]
    spec = contract("cmkq,cqdz->dzkm", spec, inverse)
    spec = lax.all_to_all(spec, "px", split_axis=1, concat_axis=3, tiled=True)
    spec = contract("cakm,cmdy->dayk", spec, inverse)
    spec = lax.all_to_all(spec, "py", split_axis=2, concat_axis=3, tiled=True)
    stress = contract("cabk,ckx->abx", spec, jnp.stack([cosines, -sine_table], 0)) / float(
        extent**3
    )
    seg_count = positions.shape[1]
    members = block_order[0]
    payload = jnp.concatenate([positions, weights[None, :]], 0)
    blocks = jnp.transpose(payload[:, members.reshape(-1, BLK)], (1, 0, 2))
    local_blocks = blocks.shape[0]
    seg_width = blocks.shape[2]
    source_local = pair_blocks[0]
    target_block = pair_blocks[1]
    destination = pair_dest[:, 0]
    pairs = destination.shape[0]
    devices = lax.psum(1, ("px", "py"))
    cap = 2
    earlier = jnp.sum(
        (destination[:, None] == destination[None, :])
        & (jnp.arange(pairs)[:, None] > jnp.arange(pairs)[None, :]),
        axis=1,
        dtype=jnp.int32,
    )
    slot = destination * cap + earlier
    wanted = jnp.zeros((devices * cap,), jnp.int32).at[slot].set(target_block)
    asked = lax.all_to_all(
        wanted.reshape(devices, cap), ("px", "py"), 0, 0, tiled=True
    ).reshape(-1)
    served = blocks[asked].reshape(devices, cap * 4 * seg_width)
    fetched = lax.all_to_all(served, ("px", "py"), 0, 0, tiled=True).reshape(
        devices * cap, 4, seg_width
    )
    on_target, on_source = evaluate(fetched[slot], blocks[source_local])
    returned = jnp.zeros((devices * cap, seg_width), jnp.float32).at[slot].set(on_target)
    arrived = lax.all_to_all(
        returned.reshape(devices, cap * seg_width), ("px", "py"), 0, 0, tiled=True
    ).reshape(devices * cap, seg_width)
    block_force = (
        jnp.zeros((local_blocks, seg_width), jnp.float32)
        .at[asked]
        .add(arrived)
        .at[source_local]
        .add(on_source)
    )
    pair_force = jnp.zeros((seg_count,), jnp.float32).at[members].set(block_force.reshape(-1))
    flat_stress = stress.reshape(-1)
    glide_force = weights * flat_stress[cell_index] + pair_force
    new_gamma = (
        gamma.reshape(-1)
        .at[cell_index]
        .add(STEP_MOBILITY * weights * glide_force)
        .reshape(gamma.shape)
    )
    return (stress, glide_force, new_gamma)


def solution(mesh):
    in_specs = (
        P("px", "py", None),
        P(None, ("px", "py")),
        P(("px", "py")),
        P(("px", "py"), None),
        P(("px", "py")),
        P(("px", "py"), None),
        P(None, ("px", "py")),
    )
    out_specs = (P("px", "py", None), P(("px", "py")), P("px", "py", None))
    return jax.shard_map(shards, mesh=mesh, in_specs=in_specs, out_specs=out_specs, check_vma=False)
```

```python
import math

import jax
import jax.numpy as jnp
from jax import lax
from jax.experimental import pallas as pl
from jax.sharding import PartitionSpec as P

BLK = 128


POISSON = 0.34
STEP_MOBILITY = 0.5
CORE_SQUARED = 1.0
ROOT_HALF = 0.7071067811865476


def wrapped(indices, number):
    shifted = jnp.where(indices == number // 2, 0, indices - number)
    return jnp.where(indices < number // 2, indices, shifted).astype(jnp.float32)


def multiplier(first, second, third):
    summed = first * first + second * second + third * third
    bounded = jnp.maximum(summed, 1.0)
    normal_part = (first + second + third) ** 2 / (3.0 * bounded)
    slip_part = (first - second) ** 2 / (2.0 * bounded)
    factor = normal_part + slip_part - 2.0 * normal_part * slip_part / (1.0 - POISSON) - 1.0
    return jnp.where(summed > 0.5, factor, 0.0)


def pair_terms(target, source):
    offset = target[:, 0:3, :, None] - source[:, 0:3, None, :]
    squared = (
        offset[:, 0] * offset[:, 0]
        + offset[:, 1] * offset[:, 1]
        + offset[:, 2] * offset[:, 2]
        + CORE_SQUARED
    )
    along = (offset[:, 0] - offset[:, 1]) * ROOT_HALF
    strength = target[:, 3, :, None] * source[:, 3, None, :]
    coupling = strength * along / (squared * jnp.sqrt(squared))
    return (jnp.sum(coupling, axis=2), -jnp.sum(coupling, axis=1))


PAIR_STEP = 32


def pair_kernel(target_ref, source_ref, on_target_ref, on_source_ref):
    columns = jnp.transpose(target_ref[...].reshape(PAIR_STEP * 4, BLK))
    source_rows = []
    target_rows = []
    for p in range(PAIR_STEP):
        source = source_ref[p]
        d0 = columns[:, 4 * p : 4 * p + 1] - source[0:1, :]
        d1 = columns[:, 4 * p + 1 : 4 * p + 2] - source[1:2, :]
        d2 = columns[:, 4 * p + 2 : 4 * p + 3] - source[2:3, :]
        squared = d0 * d0 + d1 * d1 + d2 * d2 + CORE_SQUARED
        along = (d0 - d1) * ROOT_HALF
        strength = columns[:, 4 * p + 3 : 4 * p + 4] * source[3:4, :]
        root = lax.rsqrt(squared)
        coupling = strength * along * (root * root * root)
        source_rows.append(-jnp.sum(coupling, axis=0, keepdims=True))
        target_rows.append(jnp.sum(jnp.transpose(coupling), axis=0, keepdims=True))
    on_source_ref[...] = jnp.concatenate(source_rows, 0)
    on_target_ref[...] = jnp.concatenate(target_rows, 0)


def evaluate(target, source):
    number = target.shape[0]
    width = target.shape[2]
    block_in = pl.BlockSpec((PAIR_STEP, 4, width), lambda i: (i, 0, 0))
    block_out = pl.BlockSpec((PAIR_STEP, width), lambda i: (i, 0))
    return pl.pallas_call(
        pair_kernel,
        grid=(number // PAIR_STEP,),
        in_specs=[block_in, block_in],
        out_specs=[block_out, block_out],
        out_shape=[jax.ShapeDtypeStruct((number, width), jnp.float32)] * 2,
    )(target, source)


def dft_tables(number):
    indices = jnp.arange(number, dtype=jnp.int32)
    phases = indices[:, None] * indices[None, :] % number
    angles = phases.astype(jnp.float32) * (2.0 * math.pi / number)
    return (jnp.cos(angles), jnp.sin(angles))


def contract(form, left, right):
    return jnp.einsum(form, left, right, precision=lax.Precision.HIGHEST)


def rotate(form, real_part, imag_part, cosines, sine_table, direction):
    real_out = contract(form, real_part, cosines) + direction * contract(
        form, imag_part, sine_table
    )
    imag_out = contract(form, imag_part, cosines) - direction * contract(
        form, real_part, sine_table
    )
    return (real_out, imag_out)


def across_rows(real_part, imag_part):
    return (
        lax.all_to_all(real_part, "py", split_axis=1, concat_axis=2, tiled=True),
        lax.all_to_all(imag_part, "py", split_axis=1, concat_axis=2, tiled=True),
    )


def across_columns(real_part, imag_part):
    return (
        lax.all_to_all(real_part, "px", split_axis=0, concat_axis=2, tiled=True),
        lax.all_to_all(imag_part, "px", split_axis=0, concat_axis=2, tiled=True),
    )


def cplx_table(number, direction):
    cosines, sine_table = dft_tables(number)
    top = jnp.stack([cosines, -direction * sine_table], 1)
    bottom = jnp.stack([direction * sine_table, cosines], 1)
    return jnp.stack([top, bottom], 0)


def one_hot(indices, number):
    return (indices[:, None] == jnp.arange(number, dtype=jnp.int32)[None, :]).astype(jnp.float32)


def shards(gamma, positions, weights, block_order, cell_index, pair_dest, pair_blocks):
    extent = gamma.shape[2]
    py_count = extent // gamma.shape[1]
    half = extent // 2 + 1
    kept = -(-half // py_count) * py_count
    cosines, sine_table = dft_tables(extent)
    live = (jnp.arange(kept) < half).astype(jnp.float32)
    cos_half = cosines[:, :kept] * live[None, :]
    sin_half = sine_table[:, :kept] * live[None, :]
    folds = jnp.where((jnp.arange(kept) == 0) | (jnp.arange(kept) == extent // 2), 1.0, 2.0) * live
    forward = cplx_table(extent, 1.0)
    inverse = cplx_table(extent, -1.0)
    spec = contract("abx,xck->cakb", gamma, jnp.stack([cos_half, -sin_half], 1))
    spec = lax.all_to_all(spec, "py", split_axis=2, concat_axis=3, tiled=True)
    spec = contract("caky,cydm->dmka", spec, forward)
    spec = lax.all_to_all(spec, "px", split_axis=1, concat_axis=3, tiled=True)
    spec = contract("cmkz,czdq->dmkq", spec, forward)
    rows_local = spec.shape[1]
    cols_local = spec.shape[2]
    first_index = lax.axis_index("px") * rows_local + jnp.arange(rows_local, dtype=jnp.int32)
    second_index = lax.axis_index("py") * cols_local + jnp.arange(cols_local, dtype=jnp.int32)
    third_index = jnp.arange(extent, dtype=jnp.int32)
    factor_table = multiplier(
        wrapped(third_index, extent)[None, None, :],
        wrapped(first_index, extent)[:, None, None],
        wrapped(second_index, extent)[None, :, None],
    )
    spec = spec * factor_table[None]
    spec = contract("cmkq,cqdz->dzkm", spec, inverse)
    spec = lax.all_to_all(spec, "px", split_axis=1, concat_axis=3, tiled=True)
    spec = contract("cakm,cmdy->dayk", spec, inverse)
    spec = lax.all_to_all(spec, "py", split_axis=2, concat_axis=3, tiled=True)
    final_table = jnp.stack([folds[:, None] * cos_half.T, -folds[:, None] * sin_half.T], 0)
    stress = contract("cabk,ckx->abx", spec, final_table) / float(extent**3)
    seg_count = positions.shape[1]
    members = block_order[0]
    payload = jnp.concatenate([positions, weights[None, :]], 0)
    order_hot = one_hot(members, seg_count)
    blocks = jnp.transpose(
        contract("cs,ks->ck", payload, order_hot).reshape(4, -1, BLK), (1, 0, 2)
    )
    local_blocks = blocks.shape[0]
    seg_width = blocks.shape[2]
    flat_blocks = blocks.reshape(local_blocks, 4 * seg_width)
    source_local = pair_blocks[0]
    target_block = pair_blocks[1]
    destination = pair_dest[:, 0]
    pairs = destination.shape[0]
    devices = lax.psum(1, ("px", "py"))
    cap = 2
    earlier = jnp.sum(
        (destination[:, None] == destination[None, :])
        & (jnp.arange(pairs)[:, None] > jnp.arange(pairs)[None, :]),
        axis=1,
        dtype=jnp.int32,
    )
    slot = destination * cap + earlier
    slot_match = slot[:, None] == jnp.arange(devices * cap, dtype=jnp.int32)[None, :]
    wanted = jnp.sum(jnp.where(slot_match, target_block[:, None], 0), axis=0, dtype=jnp.int32)
    asked = lax.all_to_all(
        wanted.reshape(devices, cap), ("px", "py"), 0, 0, tiled=True
    ).reshape(-1)
    asked_hot = one_hot(asked, local_blocks)
    served = contract("pb,bw->pw", asked_hot, flat_blocks).reshape(devices, cap * 4 * seg_width)
    fetched = lax.all_to_all(served, ("px", "py"), 0, 0, tiled=True).reshape(
        devices * cap, 4 * seg_width
    )
    slot_hot = slot_match.astype(jnp.float32)
    source_hot = one_hot(source_local, local_blocks)
    target_rows = contract("ps,sw->pw", slot_hot, fetched).reshape(pairs, 4, seg_width)
    source_rows = contract("pb,bw->pw", source_hot, flat_blocks).reshape(pairs, 4, seg_width)
    on_target, on_source = evaluate(target_rows, source_rows)
    returned = contract("ps,pw->sw", slot_hot, on_target)
    arrived = lax.all_to_all(
        returned.reshape(devices, cap * seg_width), ("px", "py"), 0, 0, tiled=True
    ).reshape(devices * cap, seg_width)
    block_force = contract("pb,pw->bw", asked_hot, arrived) + contract(
        "pb,pw->bw", source_hot, on_source
    )
    pair_force = contract("k,ks->s", block_force.reshape(-1), order_hot)
    rows = gamma.shape[0] * gamma.shape[1]
    row_hot = one_hot(cell_index // extent, rows)
    column_hot = one_hot(cell_index % extent, extent)
    picked = contract("sr,rc->sc", row_hot, stress.reshape(rows, extent))
    glide_force = weights * jnp.sum(picked * column_hot, axis=1) + pair_force
    update = (STEP_MOBILITY * weights * glide_force)[:, None] * column_hot
    new_gamma = (gamma.reshape(rows, extent) + contract("sr,sc->rc", row_hot, update)).reshape(
        gamma.shape
    )
    return (stress, glide_force, new_gamma)


def solution(mesh):
    in_specs = (
        P("px", "py", None),
        P(None, ("px", "py")),
        P(("px", "py")),
        P(("px", "py"), None),
        P(("px", "py")),
        P(("px", "py"), None),
        P(None, ("px", "py")),
    )
    out_specs = (P("px", "py", None), P(("px", "py")), P("px", "py", None))
    return jax.shard_map(shards, mesh=mesh, in_specs=in_specs, out_specs=out_specs, check_vma=False)
```

```python
import math

import jax
import jax.numpy as jnp
from jax import lax
from jax.experimental import pallas as pl
from jax.sharding import PartitionSpec as P

BLK = 128


POISSON = 0.34
STEP_MOBILITY = 0.5
CORE_SQUARED = 1.0
ROOT_HALF = 0.7071067811865476


def wrapped(indices, number):
    shifted = jnp.where(indices == number // 2, 0, indices - number)
    return jnp.where(indices < number // 2, indices, shifted).astype(jnp.float32)


def multiplier(first, second, third):
    summed = first * first + second * second + third * third
    bounded = jnp.maximum(summed, 1.0)
    normal_part = (first + second + third) ** 2 / (3.0 * bounded)
    slip_part = (first - second) ** 2 / (2.0 * bounded)
    factor = normal_part + slip_part - 2.0 * normal_part * slip_part / (1.0 - POISSON) - 1.0
    return jnp.where(summed > 0.5, factor, 0.0)


def pair_terms(target, source):
    offset = target[:, 0:3, :, None] - source[:, 0:3, None, :]
    squared = (
        offset[:, 0] * offset[:, 0]
        + offset[:, 1] * offset[:, 1]
        + offset[:, 2] * offset[:, 2]
        + CORE_SQUARED
    )
    along = (offset[:, 0] - offset[:, 1]) * ROOT_HALF
    strength = target[:, 3, :, None] * source[:, 3, None, :]
    coupling = strength * along / (squared * jnp.sqrt(squared))
    return (jnp.sum(coupling, axis=2), -jnp.sum(coupling, axis=1))


PAIR_STEP = 32


def pair_kernel(target_ref, source_ref, on_target_ref, on_source_ref):
    columns = jnp.transpose(target_ref[...].reshape(PAIR_STEP * 4, BLK))
    source_rows = []
    target_rows = []
    for p in range(PAIR_STEP):
        source = source_ref[p]
        d0 = columns[:, 4 * p : 4 * p + 1] - source[0:1, :]
        d1 = columns[:, 4 * p + 1 : 4 * p + 2] - source[1:2, :]
        d2 = columns[:, 4 * p + 2 : 4 * p + 3] - source[2:3, :]
        squared = d0 * d0 + d1 * d1 + d2 * d2 + CORE_SQUARED
        along = (d0 - d1) * ROOT_HALF
        strength = columns[:, 4 * p + 3 : 4 * p + 4] * source[3:4, :]
        root = lax.rsqrt(squared)
        coupling = strength * along * (root * root * root)
        source_rows.append(-jnp.sum(coupling, axis=0, keepdims=True))
        target_rows.append(jnp.sum(jnp.transpose(coupling), axis=0, keepdims=True))
    on_source_ref[...] = jnp.concatenate(source_rows, 0)
    on_target_ref[...] = jnp.concatenate(target_rows, 0)


def evaluate(target, source):
    number = target.shape[0]
    width = target.shape[2]
    block_in = pl.BlockSpec((PAIR_STEP, 4, width), lambda i: (i, 0, 0))
    block_out = pl.BlockSpec((PAIR_STEP, width), lambda i: (i, 0))
    return pl.pallas_call(
        pair_kernel,
        grid=(number // PAIR_STEP,),
        in_specs=[block_in, block_in],
        out_specs=[block_out, block_out],
        out_shape=[jax.ShapeDtypeStruct((number, width), jnp.float32)] * 2,
    )(target, source)


def dft_tables(number):
    indices = jnp.arange(number, dtype=jnp.int32)
    phases = indices[:, None] * indices[None, :] % number
    angles = phases.astype(jnp.float32) * (2.0 * math.pi / number)
    return (jnp.cos(angles), jnp.sin(angles))


def contract(form, left, right):
    return jnp.einsum(form, left, right, precision=lax.Precision.HIGHEST)


def rotate(form, real_part, imag_part, cosines, sine_table, direction):
    real_out = contract(form, real_part, cosines) + direction * contract(
        form, imag_part, sine_table
    )
    imag_out = contract(form, imag_part, cosines) - direction * contract(
        form, real_part, sine_table
    )
    return (real_out, imag_out)


def across_rows(real_part, imag_part):
    return (
        lax.all_to_all(real_part, "py", split_axis=1, concat_axis=2, tiled=True),
        lax.all_to_all(imag_part, "py", split_axis=1, concat_axis=2, tiled=True),
    )


def across_columns(real_part, imag_part):
    return (
        lax.all_to_all(real_part, "px", split_axis=0, concat_axis=2, tiled=True),
        lax.all_to_all(imag_part, "px", split_axis=0, concat_axis=2, tiled=True),
    )


def cplx_table(number, direction):
    cosines, sine_table = dft_tables(number)
    top = jnp.stack([cosines, -direction * sine_table], 1)
    bottom = jnp.stack([direction * sine_table, cosines], 1)
    return jnp.stack([top, bottom], 0)


def one_hot(indices, number):
    return (indices[:, None] == jnp.arange(number, dtype=jnp.int32)[None, :]).astype(jnp.float32)


def shards(gamma, positions, weights, block_order, cell_index, pair_dest, pair_blocks):
    extent = gamma.shape[2]
    py_count = extent // gamma.shape[1]
    half = extent // 2 + 1
    kept = -(-half // py_count) * py_count
    cosines, sine_table = dft_tables(extent)
    live = (jnp.arange(kept) < half).astype(jnp.float32)
    cos_half = cosines[:, :kept] * live[None, :]
    sin_half = sine_table[:, :kept] * live[None, :]
    folds = jnp.where((jnp.arange(kept) == 0) | (jnp.arange(kept) == extent // 2), 1.0, 2.0) * live
    forward = cplx_table(extent, 1.0)
    inverse = cplx_table(extent, -1.0)
    spec = contract("abx,xck->cakb", gamma, jnp.stack([cos_half, -sin_half], 1))
    spec = lax.all_to_all(spec, "py", split_axis=2, concat_axis=3, tiled=True)
    spec = contract("caky,cydm->dmka", spec, forward)
    spec = lax.all_to_all(spec, "px", split_axis=1, concat_axis=3, tiled=True)
    spec = contract("cmkz,czdq->dmkq", spec, forward)
    rows_local = spec.shape[1]
    cols_local = spec.shape[2]
    first_index = lax.axis_index("px") * rows_local + jnp.arange(rows_local, dtype=jnp.int32)
    second_index = lax.axis_index("py") * cols_local + jnp.arange(cols_local, dtype=jnp.int32)
    third_index = jnp.arange(extent, dtype=jnp.int32)
    factor_table = multiplier(
        wrapped(third_index, extent)[None, None, :],
        wrapped(first_index, extent)[:, None, None],
        wrapped(second_index, extent)[None, :, None],
    )
    spec = spec * factor_table[None]
    spec = contract("cmkq,cqdz->dzkm", spec, inverse)
    spec = lax.all_to_all(spec, "px", split_axis=1, concat_axis=3, tiled=True)
    spec = contract("cakm,cmdy->dayk", spec, inverse)
    spec = lax.all_to_all(spec, "py", split_axis=2, concat_axis=3, tiled=True)
    final_table = jnp.stack([folds[:, None] * cos_half.T, -folds[:, None] * sin_half.T], 0)
    stress = contract("cabk,ckx->abx", spec, final_table) / float(extent**3)
    seg_count = positions.shape[1]
    members = block_order[0]
    payload = jnp.concatenate([positions, weights[None, :]], 0)
    order_hot = one_hot(members, seg_count)
    blocks = jnp.transpose(
        contract("cs,ks->ck", payload, order_hot).reshape(4, -1, BLK), (1, 0, 2)
    )
    local_blocks = blocks.shape[0]
    seg_width = blocks.shape[2]
    flat_blocks = blocks.reshape(local_blocks, 4 * seg_width)
    source_local = pair_blocks[0]
    target_block = pair_blocks[1]
    destination = pair_dest[:, 0]
    pairs = destination.shape[0]
    devices = lax.psum(1, ("px", "py"))
    me = lax.axis_index("px") * lax.psum(1, "py") + lax.axis_index("py")
    cap = 2
    earlier = jnp.sum(
        (destination[:, None] == destination[None, :])
        & (jnp.arange(pairs)[:, None] > jnp.arange(pairs)[None, :]),
        axis=1,
        dtype=jnp.int32,
    )
    slot = destination * cap + earlier
    slot_hot = one_hot(slot, devices * cap)
    packed = jnp.concatenate(
        [
            flat_blocks.reshape(-1),
            destination.astype(jnp.float32),
            target_block.astype(jnp.float32),
        ]
    )
    gathered = lax.all_gather(packed, ("px", "py"), axis=0, tiled=False)
    block_span = local_blocks * 4 * seg_width
    every_block = gathered[:, :block_span].reshape(devices * local_blocks, 4 * seg_width)
    every_dest = gathered[:, block_span : block_span + pairs].astype(jnp.int32)
    every_target = gathered[:, block_span + pairs :].astype(jnp.int32)
    target_id = destination * local_blocks + target_block
    target_rows = every_block[target_id].reshape(pairs, 4, seg_width)
    source_hot = one_hot(source_local, local_blocks)
    source_rows = contract("pb,bw->pw", source_hot, flat_blocks).reshape(pairs, 4, seg_width)
    on_target, on_source = evaluate(target_rows, source_rows)
    returned = contract("ps,pw->sw", slot_hot, on_target)
    arrived = lax.all_to_all(
        returned.reshape(devices, cap * seg_width), ("px", "py"), 0, 0, tiled=True
    ).reshape(devices, cap, seg_width)
    mine = every_dest == me
    rank = jnp.cumsum(mine.astype(jnp.int32), axis=1) - 1
    asked_hot = jnp.stack(
        [
            jnp.sum(
                jnp.where(
                    (mine & (rank == c))[:, :, None],
                    one_hot(every_target.reshape(-1), local_blocks).reshape(devices, pairs, local_blocks),
                    0.0,
                ),
                axis=1,
            )
            for c in range(cap)
        ],
        1,
    )
    block_force = contract("dcb,dcw->bw", asked_hot, arrived) + contract(
        "pb,pw->bw", source_hot, on_source
    )
    pair_force = contract("k,ks->s", block_force.reshape(-1), order_hot)
    rows = gamma.shape[0] * gamma.shape[1]
    row_hot = one_hot(cell_index // extent, rows)
    column_hot = one_hot(cell_index % extent, extent)
    picked = contract("sr,rc->sc", row_hot, stress.reshape(rows, extent))
    glide_force = weights * jnp.sum(picked * column_hot, axis=1) + pair_force
    update = (STEP_MOBILITY * weights * glide_force)[:, None] * column_hot
    new_gamma = (gamma.reshape(rows, extent) + contract("sr,sc->rc", row_hot, update)).reshape(
        gamma.shape
    )
    return (stress, glide_force, new_gamma)


def solution(mesh):
    in_specs = (
        P("px", "py", None),
        P(None, ("px", "py")),
        P(("px", "py")),
        P(("px", "py"), None),
        P(("px", "py")),
        P(("px", "py"), None),
        P(None, ("px", "py")),
    )
    out_specs = (P("px", "py", None), P(("px", "py")), P("px", "py", None))
    return jax.shard_map(shards, mesh=mesh, in_specs=in_specs, out_specs=out_specs, check_vma=False)
```

```python
import math

import jax
import jax.numpy as jnp
from jax import lax
from jax.experimental import pallas as pl
from jax.sharding import PartitionSpec as P

BLK = 128


POISSON = 0.34
STEP_MOBILITY = 0.5
CORE_SQUARED = 1.0
ROOT_HALF = 0.7071067811865476


def wrapped(indices, number):
    shifted = jnp.where(indices == number // 2, 0, indices - number)
    return jnp.where(indices < number // 2, indices, shifted).astype(jnp.float32)


def multiplier(first, second, third):
    summed = first * first + second * second + third * third
    bounded = jnp.maximum(summed, 1.0)
    normal_part = (first + second + third) ** 2 / (3.0 * bounded)
    slip_part = (first - second) ** 2 / (2.0 * bounded)
    factor = normal_part + slip_part - 2.0 * normal_part * slip_part / (1.0 - POISSON) - 1.0
    return jnp.where(summed > 0.5, factor, 0.0)


def pair_terms(target, source):
    offset = target[:, 0:3, :, None] - source[:, 0:3, None, :]
    squared = (
        offset[:, 0] * offset[:, 0]
        + offset[:, 1] * offset[:, 1]
        + offset[:, 2] * offset[:, 2]
        + CORE_SQUARED
    )
    along = (offset[:, 0] - offset[:, 1]) * ROOT_HALF
    strength = target[:, 3, :, None] * source[:, 3, None, :]
    coupling = strength * along / (squared * jnp.sqrt(squared))
    return (jnp.sum(coupling, axis=2), -jnp.sum(coupling, axis=1))


PAIR_STEP = 32


def pair_kernel(target_ref, source_ref, on_target_ref, on_source_ref):
    columns = jnp.transpose(target_ref[...].reshape(PAIR_STEP * 4, BLK))
    source_rows = []
    target_rows = []
    for p in range(PAIR_STEP):
        source = source_ref[p]
        d0 = columns[:, 4 * p : 4 * p + 1] - source[0:1, :]
        d1 = columns[:, 4 * p + 1 : 4 * p + 2] - source[1:2, :]
        d2 = columns[:, 4 * p + 2 : 4 * p + 3] - source[2:3, :]
        squared = d0 * d0 + d1 * d1 + d2 * d2 + CORE_SQUARED
        along = (d0 - d1) * ROOT_HALF
        strength = columns[:, 4 * p + 3 : 4 * p + 4] * source[3:4, :]
        root = lax.rsqrt(squared)
        coupling = strength * along * (root * root * root)
        source_rows.append(-jnp.sum(coupling, axis=0, keepdims=True))
        target_rows.append(jnp.sum(jnp.transpose(coupling), axis=0, keepdims=True))
    on_source_ref[...] = jnp.concatenate(source_rows, 0)
    on_target_ref[...] = jnp.concatenate(target_rows, 0)


def evaluate(target, source):
    number = target.shape[0]
    width = target.shape[2]
    block_in = pl.BlockSpec((PAIR_STEP, 4, width), lambda i: (i, 0, 0))
    block_out = pl.BlockSpec((PAIR_STEP, width), lambda i: (i, 0))
    return pl.pallas_call(
        pair_kernel,
        grid=(number // PAIR_STEP,),
        in_specs=[block_in, block_in],
        out_specs=[block_out, block_out],
        out_shape=[jax.ShapeDtypeStruct((number, width), jnp.float32)] * 2,
    )(target, source)


def dft_tables(number):
    indices = jnp.arange(number, dtype=jnp.int32)
    phases = indices[:, None] * indices[None, :] % number
    angles = phases.astype(jnp.float32) * (2.0 * math.pi / number)
    return (jnp.cos(angles), jnp.sin(angles))


def contract(form, left, right):
    return jnp.einsum(form, left, right, precision=lax.Precision.HIGHEST)


def rotate(form, real_part, imag_part, cosines, sine_table, direction):
    real_out = contract(form, real_part, cosines) + direction * contract(
        form, imag_part, sine_table
    )
    imag_out = contract(form, imag_part, cosines) - direction * contract(
        form, real_part, sine_table
    )
    return (real_out, imag_out)


def across_rows(real_part, imag_part):
    return (
        lax.all_to_all(real_part, "py", split_axis=1, concat_axis=2, tiled=True),
        lax.all_to_all(imag_part, "py", split_axis=1, concat_axis=2, tiled=True),
    )


def across_columns(real_part, imag_part):
    return (
        lax.all_to_all(real_part, "px", split_axis=0, concat_axis=2, tiled=True),
        lax.all_to_all(imag_part, "px", split_axis=0, concat_axis=2, tiled=True),
    )


def cplx_table(number, direction):
    cosines, sine_table = dft_tables(number)
    top = jnp.stack([cosines, -direction * sine_table], 1)
    bottom = jnp.stack([direction * sine_table, cosines], 1)
    return jnp.stack([top, bottom], 0)


def one_hot(indices, number):
    return (indices[:, None] == jnp.arange(number, dtype=jnp.int32)[None, :]).astype(jnp.float32)


def shards(gamma, positions, weights, block_order, cell_index, pair_dest, pair_blocks):
    extent = gamma.shape[2]
    py_count = extent // gamma.shape[1]
    half = extent // 2 + 1
    kept = -(-half // py_count) * py_count
    cosines, sine_table = dft_tables(extent)
    live = (jnp.arange(kept) < half).astype(jnp.float32)
    cos_half = cosines[:, :kept] * live[None, :]
    sin_half = sine_table[:, :kept] * live[None, :]
    folds = jnp.where((jnp.arange(kept) == 0) | (jnp.arange(kept) == extent // 2), 1.0, 2.0) * live
    forward = cplx_table(extent, 1.0)
    inverse = cplx_table(extent, -1.0)
    spec = contract("abx,xck->cakb", gamma, jnp.stack([cos_half, -sin_half], 1))
    spec = lax.all_to_all(spec, "py", split_axis=2, concat_axis=3, tiled=True)
    spec = contract("caky,cydm->dmka", spec, forward)
    spec = lax.all_to_all(spec, "px", split_axis=1, concat_axis=3, tiled=True)
    spec = contract("cmkz,czdq->dmkq", spec, forward)
    rows_local = spec.shape[1]
    cols_local = spec.shape[2]
    first_index = lax.axis_index("px") * rows_local + jnp.arange(rows_local, dtype=jnp.int32)
    second_index = lax.axis_index("py") * cols_local + jnp.arange(cols_local, dtype=jnp.int32)
    third_index = jnp.arange(extent, dtype=jnp.int32)
    factor_table = multiplier(
        wrapped(third_index, extent)[None, None, :],
        wrapped(first_index, extent)[:, None, None],
        wrapped(second_index, extent)[None, :, None],
    )
    spec = spec * factor_table[None]
    spec = contract("cmkq,cqdz->dzkm", spec, inverse)
    spec = lax.all_to_all(spec, "px", split_axis=1, concat_axis=3, tiled=True)
    spec = contract("cakm,cmdy->dayk", spec, inverse)
    spec = lax.all_to_all(spec, "py", split_axis=2, concat_axis=3, tiled=True)
    final_table = jnp.stack([folds[:, None] * cos_half.T, -folds[:, None] * sin_half.T], 0)
    stress = contract("cabk,ckx->abx", spec, final_table) / float(extent**3)
    seg_count = positions.shape[1]
    members = block_order[0]
    payload = jnp.concatenate([positions, weights[None, :]], 0)
    order_hot = one_hot(members, seg_count)
    blocks = jnp.transpose(
        contract("cs,ks->ck", payload, order_hot).reshape(4, -1, BLK), (1, 0, 2)
    )
    local_blocks = blocks.shape[0]
    seg_width = blocks.shape[2]
    flat_blocks = blocks.reshape(local_blocks, 4 * seg_width)
    source_local = pair_blocks[0]
    target_block = pair_blocks[1]
    destination = pair_dest[:, 0]
    pairs = destination.shape[0]
    devices = lax.psum(1, ("px", "py"))
    me = lax.axis_index("px") * lax.psum(1, "py") + lax.axis_index("py")
    cap = 2
    earlier = jnp.sum(
        (destination[:, None] == destination[None, :])
        & (jnp.arange(pairs)[:, None] > jnp.arange(pairs)[None, :]),
        axis=1,
        dtype=jnp.int32,
    )
    slot = destination * cap + earlier
    slot_hot = one_hot(slot, devices * cap)
    table_row = jnp.concatenate([destination, target_block]).astype(jnp.float32)
    everything = lax.all_gather(
        jnp.concatenate([flat_blocks, table_row[None, :]], 0), ("px", "py"), axis=0, tiled=True
    )
    stride = local_blocks + 1
    tables = everything.reshape(devices, stride, 2 * pairs)[:, local_blocks, :].astype(jnp.int32)
    every_dest = tables[:, :pairs]
    every_target = tables[:, pairs:]
    target_rows = everything[destination * stride + target_block].reshape(pairs, 4, seg_width)
    source_hot = one_hot(source_local, local_blocks)
    source_rows = contract("pb,bw->pw", source_hot, flat_blocks).reshape(pairs, 4, seg_width)
    on_target, on_source = evaluate(target_rows, source_rows)
    returned = contract("ps,pw->sw", slot_hot, on_target)
    arrived = lax.all_to_all(
        returned.reshape(devices, cap * seg_width), ("px", "py"), 0, 0, tiled=True
    ).reshape(devices, cap, seg_width)
    mine = every_dest == me
    rank = jnp.cumsum(mine.astype(jnp.int32), axis=1) - 1
    asked_hot = jnp.stack(
        [
            jnp.sum(
                jnp.where(
                    (mine & (rank == c))[:, :, None],
                    one_hot(every_target.reshape(-1), local_blocks).reshape(devices, pairs, local_blocks),
                    0.0,
                ),
                axis=1,
            )
            for c in range(cap)
        ],
        1,
    )
    block_force = contract("dcb,dcw->bw", asked_hot, arrived) + contract(
        "pb,pw->bw", source_hot, on_source
    )
    pair_force = contract("k,ks->s", block_force.reshape(-1), order_hot)
    rows = gamma.shape[0] * gamma.shape[1]
    row_hot = one_hot(cell_index // extent, rows)
    column_hot = one_hot(cell_index % extent, extent)
    picked = contract("sr,rc->sc", row_hot, stress.reshape(rows, extent))
    glide_force = weights * jnp.sum(picked * column_hot, axis=1) + pair_force
    update = (STEP_MOBILITY * weights * glide_force)[:, None] * column_hot
    new_gamma = (gamma.reshape(rows, extent) + contract("sr,sc->rc", row_hot, update)).reshape(
        gamma.shape
    )
    return (stress, glide_force, new_gamma)


def solution(mesh):
    in_specs = (
        P("px", "py", None),
        P(None, ("px", "py")),
        P(("px", "py")),
        P(("px", "py"), None),
        P(("px", "py")),
        P(("px", "py"), None),
        P(None, ("px", "py")),
    )
    out_specs = (P("px", "py", None), P(("px", "py")), P("px", "py", None))
    return jax.shard_map(shards, mesh=mesh, in_specs=in_specs, out_specs=out_specs, check_vma=False)
```

```python
import math

import jax
import jax.numpy as jnp
from jax import lax
from jax.experimental import pallas as pl
from jax.sharding import PartitionSpec as P

BLK = 128


POISSON = 0.34
STEP_MOBILITY = 0.5
CORE_SQUARED = 1.0
ROOT_HALF = 0.7071067811865476


def wrapped(indices, number):
    shifted = jnp.where(indices == number // 2, 0, indices - number)
    return jnp.where(indices < number // 2, indices, shifted).astype(jnp.float32)


def multiplier(first, second, third):
    summed = first * first + second * second + third * third
    bounded = jnp.maximum(summed, 1.0)
    normal_part = (first + second + third) ** 2 / (3.0 * bounded)
    slip_part = (first - second) ** 2 / (2.0 * bounded)
    factor = normal_part + slip_part - 2.0 * normal_part * slip_part / (1.0 - POISSON) - 1.0
    return jnp.where(summed > 0.5, factor, 0.0)


def pair_terms(target, source):
    offset = target[:, 0:3, :, None] - source[:, 0:3, None, :]
    squared = (
        offset[:, 0] * offset[:, 0]
        + offset[:, 1] * offset[:, 1]
        + offset[:, 2] * offset[:, 2]
        + CORE_SQUARED
    )
    along = (offset[:, 0] - offset[:, 1]) * ROOT_HALF
    strength = target[:, 3, :, None] * source[:, 3, None, :]
    coupling = strength * along / (squared * jnp.sqrt(squared))
    return (jnp.sum(coupling, axis=2), -jnp.sum(coupling, axis=1))


PAIR_STEP = 32


def pair_kernel(target_ref, source_ref, on_target_ref, on_source_ref):
    columns = jnp.transpose(target_ref[...].reshape(PAIR_STEP * 4, BLK))
    source_rows = []
    target_rows = []
    for p in range(PAIR_STEP):
        source = source_ref[p]
        d0 = columns[:, 4 * p : 4 * p + 1] - source[0:1, :]
        d1 = columns[:, 4 * p + 1 : 4 * p + 2] - source[1:2, :]
        d2 = columns[:, 4 * p + 2 : 4 * p + 3] - source[2:3, :]
        squared = d0 * d0 + d1 * d1 + d2 * d2 + CORE_SQUARED
        along = (d0 - d1) * ROOT_HALF
        strength = columns[:, 4 * p + 3 : 4 * p + 4] * source[3:4, :]
        root = lax.rsqrt(squared)
        coupling = strength * along * (root * root * root)
        source_rows.append(-jnp.sum(coupling, axis=0, keepdims=True))
        target_rows.append(jnp.sum(jnp.transpose(coupling), axis=0, keepdims=True))
    on_source_ref[...] = jnp.concatenate(source_rows, 0)
    on_target_ref[...] = jnp.concatenate(target_rows, 0)


def evaluate(target, source):
    number = target.shape[0]
    width = target.shape[2]
    block_in = pl.BlockSpec((PAIR_STEP, 4, width), lambda i: (i, 0, 0))
    block_out = pl.BlockSpec((PAIR_STEP, width), lambda i: (i, 0))
    return pl.pallas_call(
        pair_kernel,
        grid=(number // PAIR_STEP,),
        in_specs=[block_in, block_in],
        out_specs=[block_out, block_out],
        out_shape=[jax.ShapeDtypeStruct((number, width), jnp.float32)] * 2,
    )(target, source)


def dft_tables(number):
    indices = jnp.arange(number, dtype=jnp.int32)
    phases = indices[:, None] * indices[None, :] % number
    angles = phases.astype(jnp.float32) * (2.0 * math.pi / number)
    return (jnp.cos(angles), jnp.sin(angles))


def contract(form, left, right):
    return jnp.einsum(form, left, right, precision=lax.Precision.HIGHEST)


def rotate(form, real_part, imag_part, cosines, sine_table, direction):
    real_out = contract(form, real_part, cosines) + direction * contract(
        form, imag_part, sine_table
    )
    imag_out = contract(form, imag_part, cosines) - direction * contract(
        form, real_part, sine_table
    )
    return (real_out, imag_out)


def across_rows(real_part, imag_part):
    return (
        lax.all_to_all(real_part, "py", split_axis=1, concat_axis=2, tiled=True),
        lax.all_to_all(imag_part, "py", split_axis=1, concat_axis=2, tiled=True),
    )


def across_columns(real_part, imag_part):
    return (
        lax.all_to_all(real_part, "px", split_axis=0, concat_axis=2, tiled=True),
        lax.all_to_all(imag_part, "px", split_axis=0, concat_axis=2, tiled=True),
    )


def cplx_table(number, direction):
    cosines, sine_table = dft_tables(number)
    top = jnp.stack([cosines, -direction * sine_table], 1)
    bottom = jnp.stack([direction * sine_table, cosines], 1)
    return jnp.stack([top, bottom], 0)


def one_hot(indices, number):
    return (indices[:, None] == jnp.arange(number, dtype=jnp.int32)[None, :]).astype(jnp.float32)


def shards(gamma, positions, weights, block_order, cell_index, pair_dest, pair_blocks):
    extent = gamma.shape[2]
    py_count = extent // gamma.shape[1]
    half = extent // 2 + 1
    kept = -(-half // py_count) * py_count
    cosines, sine_table = dft_tables(extent)
    live = (jnp.arange(kept) < half).astype(jnp.float32)
    cos_half = cosines[:, :kept] * live[None, :]
    sin_half = sine_table[:, :kept] * live[None, :]
    folds = jnp.where((jnp.arange(kept) == 0) | (jnp.arange(kept) == extent // 2), 1.0, 2.0) * live
    forward = cplx_table(extent, 1.0)
    inverse = cplx_table(extent, -1.0)
    spec = contract("abx,xck->cakb", gamma, jnp.stack([cos_half, -sin_half], 1))
    spec = lax.all_to_all(spec, "py", split_axis=2, concat_axis=3, tiled=True)
    spec = contract("caky,cydm->dmka", spec, forward)
    spec = lax.all_to_all(spec, "px", split_axis=1, concat_axis=3, tiled=True)
    spec = contract("cmkz,czdq->dmkq", spec, forward)
    rows_local = spec.shape[1]
    cols_local = spec.shape[2]
    first_index = lax.axis_index("px") * rows_local + jnp.arange(rows_local, dtype=jnp.int32)
    second_index = lax.axis_index("py") * cols_local + jnp.arange(cols_local, dtype=jnp.int32)
    third_index = jnp.arange(extent, dtype=jnp.int32)
    factor_table = multiplier(
        wrapped(third_index, extent)[None, None, :],
        wrapped(first_index, extent)[:, None, None],
        wrapped(second_index, extent)[None, :, None],
    )
    spec = spec * factor_table[None]
    spec = contract("cmkq,cqdz->dzkm", spec, inverse)
    spec = lax.all_to_all(spec, "px", split_axis=1, concat_axis=3, tiled=True)
    spec = contract("cakm,cmdy->dayk", spec, inverse)
    spec = lax.all_to_all(spec, "py", split_axis=2, concat_axis=3, tiled=True)
    final_table = jnp.stack([folds[:, None] * cos_half.T, -folds[:, None] * sin_half.T], 0)
    stress = contract("cabk,ckx->abx", spec, final_table) / float(extent**3)
    seg_count = positions.shape[1]
    members = block_order[0]
    payload = jnp.concatenate([positions, weights[None, :]], 0)
    order_hot = one_hot(members, seg_count)
    blocks = jnp.transpose(
        contract("cs,ks->ck", payload, order_hot).reshape(4, -1, BLK), (1, 0, 2)
    )
    local_blocks = blocks.shape[0]
    seg_width = blocks.shape[2]
    flat_blocks = blocks.reshape(local_blocks, 4 * seg_width)
    source_local = pair_blocks[0]
    target_block = pair_blocks[1]
    destination = pair_dest[:, 0]
    pairs = destination.shape[0]
    devices = lax.psum(1, ("px", "py"))
    cap = 2
    earlier = jnp.sum(
        (destination[:, None] == destination[None, :])
        & (jnp.arange(pairs)[:, None] > jnp.arange(pairs)[None, :]),
        axis=1,
        dtype=jnp.int32,
    )
    slot = destination * cap + earlier
    slot_match = slot[:, None] == jnp.arange(devices * cap, dtype=jnp.int32)[None, :]
    me = lax.axis_index("px") * lax.psum(1, "py") + lax.axis_index("py")
    tables = lax.all_gather(
        jnp.concatenate([destination, target_block]).astype(jnp.float32)[None, :],
        ("px", "py"),
        axis=0,
        tiled=True,
    ).astype(jnp.int32)
    mine = tables[:, :pairs] == me
    rank = jnp.cumsum(mine.astype(jnp.int32), axis=1) - 1
    asked = jnp.stack(
        [jnp.sum(jnp.where(mine & (rank == c), tables[:, pairs:], 0), axis=1) for c in range(cap)], 1
    ).reshape(-1)
    asked_hot = one_hot(asked, local_blocks)
    served = contract("pb,bw->pw", asked_hot, flat_blocks).reshape(devices, cap * 4 * seg_width)
    fetched = lax.all_to_all(served, ("px", "py"), 0, 0, tiled=True).reshape(
        devices * cap, 4 * seg_width
    )
    slot_hot = slot_match.astype(jnp.float32)
    source_hot = one_hot(source_local, local_blocks)
    target_rows = contract("ps,sw->pw", slot_hot, fetched).reshape(pairs, 4, seg_width)
    source_rows = contract("pb,bw->pw", source_hot, flat_blocks).reshape(pairs, 4, seg_width)
    on_target, on_source = evaluate(target_rows, source_rows)
    returned = contract("ps,pw->sw", slot_hot, on_target)
    arrived = lax.all_to_all(
        returned.reshape(devices, cap * seg_width), ("px", "py"), 0, 0, tiled=True
    ).reshape(devices * cap, seg_width)
    block_force = contract("pb,pw->bw", asked_hot, arrived) + contract(
        "pb,pw->bw", source_hot, on_source
    )
    pair_force = contract("k,ks->s", block_force.reshape(-1), order_hot)
    rows = gamma.shape[0] * gamma.shape[1]
    row_hot = one_hot(cell_index // extent, rows)
    column_hot = one_hot(cell_index % extent, extent)
    picked = contract("sr,rc->sc", row_hot, stress.reshape(rows, extent))
    glide_force = weights * jnp.sum(picked * column_hot, axis=1) + pair_force
    update = (STEP_MOBILITY * weights * glide_force)[:, None] * column_hot
    new_gamma = (gamma.reshape(rows, extent) + contract("sr,sc->rc", row_hot, update)).reshape(
        gamma.shape
    )
    return (stress, glide_force, new_gamma)


def solution(mesh):
    in_specs = (
        P("px", "py", None),
        P(None, ("px", "py")),
        P(("px", "py")),
        P(("px", "py"), None),
        P(("px", "py")),
        P(("px", "py"), None),
        P(None, ("px", "py")),
    )
    out_specs = (P("px", "py", None), P(("px", "py")), P("px", "py", None))
    return jax.shard_map(shards, mesh=mesh, in_specs=in_specs, out_specs=out_specs, check_vma=False)
```

```python
import math

import jax
import jax.numpy as jnp
from jax import lax
from jax.experimental import pallas as pl
from jax.sharding import PartitionSpec as P

BLK = 128


POISSON = 0.34
STEP_MOBILITY = 0.5
CORE_SQUARED = 1.0
ROOT_HALF = 0.7071067811865476


def wrapped(indices, number):
    shifted = jnp.where(indices == number // 2, 0, indices - number)
    return jnp.where(indices < number // 2, indices, shifted).astype(jnp.float32)


def multiplier(first, second, third):
    summed = first * first + second * second + third * third
    bounded = jnp.maximum(summed, 1.0)
    normal_part = (first + second + third) ** 2 / (3.0 * bounded)
    slip_part = (first - second) ** 2 / (2.0 * bounded)
    factor = normal_part + slip_part - 2.0 * normal_part * slip_part / (1.0 - POISSON) - 1.0
    return jnp.where(summed > 0.5, factor, 0.0)


def pair_terms(target, source):
    offset = target[:, 0:3, :, None] - source[:, 0:3, None, :]
    squared = (
        offset[:, 0] * offset[:, 0]
        + offset[:, 1] * offset[:, 1]
        + offset[:, 2] * offset[:, 2]
        + CORE_SQUARED
    )
    along = (offset[:, 0] - offset[:, 1]) * ROOT_HALF
    strength = target[:, 3, :, None] * source[:, 3, None, :]
    coupling = strength * along / (squared * jnp.sqrt(squared))
    return (jnp.sum(coupling, axis=2), -jnp.sum(coupling, axis=1))


PAIR_STEP = 32


def pair_kernel(target_ref, source_ref, on_target_ref, on_source_ref):
    columns = jnp.transpose(target_ref[...].reshape(PAIR_STEP * 4, BLK))
    source_rows = []
    target_rows = []
    for p in range(PAIR_STEP):
        source = source_ref[p]
        d0 = columns[:, 4 * p : 4 * p + 1] - source[0:1, :]
        d1 = columns[:, 4 * p + 1 : 4 * p + 2] - source[1:2, :]
        d2 = columns[:, 4 * p + 2 : 4 * p + 3] - source[2:3, :]
        squared = d0 * d0 + d1 * d1 + d2 * d2 + CORE_SQUARED
        along = (d0 - d1) * ROOT_HALF
        strength = columns[:, 4 * p + 3 : 4 * p + 4] * source[3:4, :]
        root = lax.rsqrt(squared)
        coupling = strength * along * (root * root * root)
        source_rows.append(-jnp.sum(coupling, axis=0, keepdims=True))
        high = coupling.astype(jnp.bfloat16)
        low = (coupling - high.astype(jnp.float32)).astype(jnp.bfloat16)
        ones = jnp.ones((8, BLK), jnp.bfloat16)
        lanes = (((1,), (1,)), ((), ()))
        sums = lax.dot_general(
            ones, high, lanes, preferred_element_type=jnp.float32
        ) + lax.dot_general(ones, low, lanes, preferred_element_type=jnp.float32)
        target_rows.append(sums[0:1, :])
    on_source_ref[...] = jnp.concatenate(source_rows, 0)
    on_target_ref[...] = jnp.concatenate(target_rows, 0)


def evaluate(target, source):
    number = target.shape[0]
    width = target.shape[2]
    block_in = pl.BlockSpec((PAIR_STEP, 4, width), lambda i: (i, 0, 0))
    block_out = pl.BlockSpec((PAIR_STEP, width), lambda i: (i, 0))
    return pl.pallas_call(
        pair_kernel,
        grid=(number // PAIR_STEP,),
        in_specs=[block_in, block_in],
        out_specs=[block_out, block_out],
        out_shape=[jax.ShapeDtypeStruct((number, width), jnp.float32)] * 2,
    )(target, source)


def dft_tables(number):
    indices = jnp.arange(number, dtype=jnp.int32)
    phases = indices[:, None] * indices[None, :] % number
    angles = phases.astype(jnp.float32) * (2.0 * math.pi / number)
    return (jnp.cos(angles), jnp.sin(angles))


def contract(form, left, right):
    return jnp.einsum(form, left, right, precision=lax.Precision.HIGHEST)


def rotate(form, real_part, imag_part, cosines, sine_table, direction):
    real_out = contract(form, real_part, cosines) + direction * contract(
        form, imag_part, sine_table
    )
    imag_out = contract(form, imag_part, cosines) - direction * contract(
        form, real_part, sine_table
    )
    return (real_out, imag_out)


def across_rows(real_part, imag_part):
    return (
        lax.all_to_all(real_part, "py", split_axis=1, concat_axis=2, tiled=True),
        lax.all_to_all(imag_part, "py", split_axis=1, concat_axis=2, tiled=True),
    )


def across_columns(real_part, imag_part):
    return (
        lax.all_to_all(real_part, "px", split_axis=0, concat_axis=2, tiled=True),
        lax.all_to_all(imag_part, "px", split_axis=0, concat_axis=2, tiled=True),
    )


def cplx_table(number, direction):
    cosines, sine_table = dft_tables(number)
    top = jnp.stack([cosines, -direction * sine_table], 1)
    bottom = jnp.stack([direction * sine_table, cosines], 1)
    return jnp.stack([top, bottom], 0)


def one_hot(indices, number):
    return (indices[:, None] == jnp.arange(number, dtype=jnp.int32)[None, :]).astype(jnp.float32)


def shards(gamma, positions, weights, block_order, cell_index, pair_dest, pair_blocks):
    extent = gamma.shape[2]
    py_count = extent // gamma.shape[1]
    half = extent // 2 + 1
    kept = -(-half // py_count) * py_count
    cosines, sine_table = dft_tables(extent)
    live = (jnp.arange(kept) < half).astype(jnp.float32)
    cos_half = cosines[:, :kept] * live[None, :]
    sin_half = sine_table[:, :kept] * live[None, :]
    folds = jnp.where((jnp.arange(kept) == 0) | (jnp.arange(kept) == extent // 2), 1.0, 2.0) * live
    forward = cplx_table(extent, 1.0)
    inverse = cplx_table(extent, -1.0)
    spec = contract("abx,xck->cakb", gamma, jnp.stack([cos_half, -sin_half], 1))
    spec = lax.all_to_all(spec, "py", split_axis=2, concat_axis=3, tiled=True)
    spec = contract("caky,cydm->dmka", spec, forward)
    spec = lax.all_to_all(spec, "px", split_axis=1, concat_axis=3, tiled=True)
    spec = contract("cmkz,czdq->dmkq", spec, forward)
    rows_local = spec.shape[1]
    cols_local = spec.shape[2]
    first_index = lax.axis_index("px") * rows_local + jnp.arange(rows_local, dtype=jnp.int32)
    second_index = lax.axis_index("py") * cols_local + jnp.arange(cols_local, dtype=jnp.int32)
    third_index = jnp.arange(extent, dtype=jnp.int32)
    factor_table = multiplier(
        wrapped(third_index, extent)[None, None, :],
        wrapped(first_index, extent)[:, None, None],
        wrapped(second_index, extent)[None, :, None],
    )
    spec = spec * factor_table[None]
    spec = contract("cmkq,cqdz->dzkm", spec, inverse)
    spec = lax.all_to_all(spec, "px", split_axis=1, concat_axis=3, tiled=True)
    spec = contract("cakm,cmdy->dayk", spec, inverse)
    spec = lax.all_to_all(spec, "py", split_axis=2, concat_axis=3, tiled=True)
    final_table = jnp.stack([folds[:, None] * cos_half.T, -folds[:, None] * sin_half.T], 0)
    stress = contract("cabk,ckx->abx", spec, final_table) / float(extent**3)
    seg_count = positions.shape[1]
    members = block_order[0]
    payload = jnp.concatenate([positions, weights[None, :]], 0)
    order_hot = one_hot(members, seg_count)
    blocks = jnp.transpose(
        contract("cs,ks->ck", payload, order_hot).reshape(4, -1, BLK), (1, 0, 2)
    )
    local_blocks = blocks.shape[0]
    seg_width = blocks.shape[2]
    flat_blocks = blocks.reshape(local_blocks, 4 * seg_width)
    source_local = pair_blocks[0]
    target_block = pair_blocks[1]
    destination = pair_dest[:, 0]
    pairs = destination.shape[0]
    devices = lax.psum(1, ("px", "py"))
    cap = 2
    earlier = jnp.sum(
        (destination[:, None] == destination[None, :])
        & (jnp.arange(pairs)[:, None] > jnp.arange(pairs)[None, :]),
        axis=1,
        dtype=jnp.int32,
    )
    slot = destination * cap + earlier
    slot_match = slot[:, None] == jnp.arange(devices * cap, dtype=jnp.int32)[None, :]
    wanted = jnp.sum(jnp.where(slot_match, target_block[:, None], 0), axis=0, dtype=jnp.int32)
    asked = lax.all_to_all(
        wanted.reshape(devices, cap), ("px", "py"), 0, 0, tiled=True
    ).reshape(-1)
    asked_hot = one_hot(asked, local_blocks)
    served = contract("pb,bw->pw", asked_hot, flat_blocks).reshape(devices, cap * 4 * seg_width)
    fetched = lax.all_to_all(served, ("px", "py"), 0, 0, tiled=True).reshape(
        devices * cap, 4 * seg_width
    )
    slot_hot = slot_match.astype(jnp.float32)
    source_hot = one_hot(source_local, local_blocks)
    target_rows = contract("ps,sw->pw", slot_hot, fetched).reshape(pairs, 4, seg_width)
    source_rows = contract("pb,bw->pw", source_hot, flat_blocks).reshape(pairs, 4, seg_width)
    on_target, on_source = evaluate(target_rows, source_rows)
    returned = contract("ps,pw->sw", slot_hot, on_target)
    arrived = lax.all_to_all(
        returned.reshape(devices, cap * seg_width), ("px", "py"), 0, 0, tiled=True
    ).reshape(devices * cap, seg_width)
    block_force = contract("pb,pw->bw", asked_hot, arrived) + contract(
        "pb,pw->bw", source_hot, on_source
    )
    pair_force = contract("k,ks->s", block_force.reshape(-1), order_hot)
    rows = gamma.shape[0] * gamma.shape[1]
    row_hot = one_hot(cell_index // extent, rows)
    column_hot = one_hot(cell_index % extent, extent)
    picked = contract("sr,rc->sc", row_hot, stress.reshape(rows, extent))
    glide_force = weights * jnp.sum(picked * column_hot, axis=1) + pair_force
    update = (STEP_MOBILITY * weights * glide_force)[:, None] * column_hot
    new_gamma = (gamma.reshape(rows, extent) + contract("sr,sc->rc", row_hot, update)).reshape(
        gamma.shape
    )
    return (stress, glide_force, new_gamma)


def solution(mesh):
    in_specs = (
        P("px", "py", None),
        P(None, ("px", "py")),
        P(("px", "py")),
        P(("px", "py"), None),
        P(("px", "py")),
        P(("px", "py"), None),
        P(None, ("px", "py")),
    )
    out_specs = (P("px", "py", None), P(("px", "py")), P("px", "py", None))
    return jax.shard_map(shards, mesh=mesh, in_specs=in_specs, out_specs=out_specs, check_vma=False)
```

```python
import math

import jax
import jax.numpy as jnp
from jax import lax
from jax.experimental import pallas as pl
from jax.sharding import PartitionSpec as P

BLK = 128


POISSON = 0.34
STEP_MOBILITY = 0.5
CORE_SQUARED = 1.0
ROOT_HALF = 0.7071067811865476


def wrapped(indices, number):
    shifted = jnp.where(indices == number // 2, 0, indices - number)
    return jnp.where(indices < number // 2, indices, shifted).astype(jnp.float32)


def multiplier(first, second, third):
    summed = first * first + second * second + third * third
    bounded = jnp.maximum(summed, 1.0)
    normal_part = (first + second + third) ** 2 / (3.0 * bounded)
    slip_part = (first - second) ** 2 / (2.0 * bounded)
    factor = normal_part + slip_part - 2.0 * normal_part * slip_part / (1.0 - POISSON) - 1.0
    return jnp.where(summed > 0.5, factor, 0.0)


def pair_terms(target, source):
    offset = target[:, 0:3, :, None] - source[:, 0:3, None, :]
    squared = (
        offset[:, 0] * offset[:, 0]
        + offset[:, 1] * offset[:, 1]
        + offset[:, 2] * offset[:, 2]
        + CORE_SQUARED
    )
    along = (offset[:, 0] - offset[:, 1]) * ROOT_HALF
    strength = target[:, 3, :, None] * source[:, 3, None, :]
    coupling = strength * along / (squared * jnp.sqrt(squared))
    return (jnp.sum(coupling, axis=2), -jnp.sum(coupling, axis=1))


PAIR_STEP = 32


def pair_kernel(target_ref, source_ref, on_target_ref, on_source_ref):
    columns = jnp.transpose(target_ref[...].reshape(PAIR_STEP * 4, BLK))
    source_rows = []
    target_rows = []
    for p in range(PAIR_STEP):
        source = source_ref[p]
        d0 = columns[:, 4 * p : 4 * p + 1] - source[0:1, :]
        d1 = columns[:, 4 * p + 1 : 4 * p + 2] - source[1:2, :]
        d2 = columns[:, 4 * p + 2 : 4 * p + 3] - source[2:3, :]
        squared = d0 * d0 + d1 * d1 + d2 * d2 + CORE_SQUARED
        along = (d0 - d1) * ROOT_HALF
        strength = columns[:, 4 * p + 3 : 4 * p + 4] * source[3:4, :]
        root = lax.rsqrt(squared)
        coupling = strength * along * (root * root * root)
        source_rows.append(-jnp.sum(coupling, axis=0, keepdims=True))
        high = coupling.astype(jnp.bfloat16)
        low = (coupling - high.astype(jnp.float32)).astype(jnp.bfloat16)
        ones = jnp.ones((8, BLK), jnp.bfloat16)
        lanes = (((1,), (1,)), ((), ()))
        sums = lax.dot_general(
            ones, high, lanes, preferred_element_type=jnp.float32
        ) + lax.dot_general(ones, low, lanes, preferred_element_type=jnp.float32)
        target_rows.append(sums[0:1, :])
    on_source_ref[...] = jnp.concatenate(source_rows, 0)
    on_target_ref[...] = jnp.concatenate(target_rows, 0)


def evaluate(target, source):
    number = target.shape[0]
    width = target.shape[2]
    block_in = pl.BlockSpec((PAIR_STEP, 4, width), lambda i: (i, 0, 0))
    block_out = pl.BlockSpec((PAIR_STEP, width), lambda i: (i, 0))
    return pl.pallas_call(
        pair_kernel,
        grid=(number // PAIR_STEP,),
        in_specs=[block_in, block_in],
        out_specs=[block_out, block_out],
        out_shape=[jax.ShapeDtypeStruct((number, width), jnp.float32)] * 2,
    )(target, source)


def dft_tables(number):
    indices = jnp.arange(number, dtype=jnp.int32)
    phases = indices[:, None] * indices[None, :] % number
    angles = phases.astype(jnp.float32) * (2.0 * math.pi / number)
    return (jnp.cos(angles), jnp.sin(angles))


def contract(form, left, right):
    return jnp.einsum(form, left, right, precision=lax.Precision.HIGHEST)


def rotate(form, real_part, imag_part, cosines, sine_table, direction):
    real_out = contract(form, real_part, cosines) + direction * contract(
        form, imag_part, sine_table
    )
    imag_out = contract(form, imag_part, cosines) - direction * contract(
        form, real_part, sine_table
    )
    return (real_out, imag_out)


def across_rows(real_part, imag_part):
    return (
        lax.all_to_all(real_part, "py", split_axis=1, concat_axis=2, tiled=True),
        lax.all_to_all(imag_part, "py", split_axis=1, concat_axis=2, tiled=True),
    )


def across_columns(real_part, imag_part):
    return (
        lax.all_to_all(real_part, "px", split_axis=0, concat_axis=2, tiled=True),
        lax.all_to_all(imag_part, "px", split_axis=0, concat_axis=2, tiled=True),
    )


def cplx_table(number, direction):
    cosines, sine_table = dft_tables(number)
    top = jnp.stack([cosines, -direction * sine_table], 1)
    bottom = jnp.stack([direction * sine_table, cosines], 1)
    return jnp.stack([top, bottom], 0)


def one_hot(indices, number):
    return (indices[:, None] == jnp.arange(number, dtype=jnp.int32)[None, :]).astype(jnp.float32)


def shards(gamma, positions, weights, block_order, cell_index, pair_dest, pair_blocks):
    extent = gamma.shape[2]
    py_count = extent // gamma.shape[1]
    half = extent // 2 + 1
    kept = -(-half // py_count) * py_count
    cosines, sine_table = dft_tables(extent)
    live = (jnp.arange(kept) < half).astype(jnp.float32)
    cos_half = cosines[:, :kept] * live[None, :]
    sin_half = sine_table[:, :kept] * live[None, :]
    folds = jnp.where((jnp.arange(kept) == 0) | (jnp.arange(kept) == extent // 2), 1.0, 2.0) * live
    forward = cplx_table(extent, 1.0)
    inverse = cplx_table(extent, -1.0)
    destination = pair_dest[:, 0]
    target_block = pair_blocks[1]
    pairs = destination.shape[0]
    devices = lax.psum(1, ("px", "py"))
    px_count = devices // py_count
    cap = 2
    earlier = jnp.sum(
        (destination[:, None] == destination[None, :])
        & (jnp.arange(pairs)[:, None] > jnp.arange(pairs)[None, :]),
        axis=1,
        dtype=jnp.int32,
    )
    slot = destination * cap + earlier
    slot_match = slot[:, None] == jnp.arange(devices * cap, dtype=jnp.int32)[None, :]
    wanted = jnp.sum(jnp.where(slot_match, target_block[:, None], 0), axis=0, dtype=jnp.int32)
    wanted = wanted.astype(jnp.float32).reshape(px_count, py_count, cap)
    spec = contract("abx,xck->cakb", gamma, jnp.stack([cos_half, -sin_half], 1))
    c2, a2, k2, b2 = spec.shape
    sent = jnp.transpose(spec.reshape(c2, a2, py_count, k2 // py_count, b2), (2, 0, 1, 3, 4))
    sent = jnp.concatenate(
        [sent.reshape(py_count, -1), jnp.transpose(wanted, (1, 0, 2)).reshape(py_count, -1)], 1
    )
    got = lax.all_to_all(sent, "py", 0, 0, tiled=True)
    body = c2 * a2 * (k2 // py_count) * b2
    spec = jnp.transpose(
        got[:, :body].reshape(py_count, c2, a2, k2 // py_count, b2), (1, 2, 3, 0, 4)
    ).reshape(c2, a2, k2 // py_count, py_count * b2)
    relay = got[:, body:].reshape(py_count, px_count, cap)
    spec = contract("caky,cydm->dmka", spec, forward)
    c3, m3, k3, a3 = spec.shape
    sent = jnp.transpose(spec.reshape(c3, px_count, m3 // px_count, k3, a3), (1, 0, 2, 3, 4))
    sent = jnp.concatenate(
        [sent.reshape(px_count, -1), jnp.transpose(relay, (1, 0, 2)).reshape(px_count, -1)], 1
    )
    got = lax.all_to_all(sent, "px", 0, 0, tiled=True)
    body = c3 * (m3 // px_count) * k3 * a3
    spec = jnp.transpose(
        got[:, :body].reshape(px_count, c3, m3 // px_count, k3, a3), (1, 2, 3, 0, 4)
    ).reshape(c3, m3 // px_count, k3, px_count * a3)
    asked = got[:, body:].reshape(-1).astype(jnp.int32)
    spec = contract("cmkz,czdq->dmkq", spec, forward)
    rows_local = spec.shape[1]
    cols_local = spec.shape[2]
    first_index = lax.axis_index("px") * rows_local + jnp.arange(rows_local, dtype=jnp.int32)
    second_index = lax.axis_index("py") * cols_local + jnp.arange(cols_local, dtype=jnp.int32)
    third_index = jnp.arange(extent, dtype=jnp.int32)
    factor_table = multiplier(
        wrapped(third_index, extent)[None, None, :],
        wrapped(first_index, extent)[:, None, None],
        wrapped(second_index, extent)[None, :, None],
    )
    spec = spec * factor_table[None]
    spec = contract("cmkq,cqdz->dzkm", spec, inverse)
    spec = lax.all_to_all(spec, "px", split_axis=1, concat_axis=3, tiled=True)
    spec = contract("cakm,cmdy->dayk", spec, inverse)
    spec = lax.all_to_all(spec, "py", split_axis=2, concat_axis=3, tiled=True)
    final_table = jnp.stack([folds[:, None] * cos_half.T, -folds[:, None] * sin_half.T], 0)
    stress = contract("cabk,ckx->abx", spec, final_table) / float(extent**3)
    seg_count = positions.shape[1]
    members = block_order[0]
    payload = jnp.concatenate([positions, weights[None, :]], 0)
    order_hot = one_hot(members, seg_count)
    blocks = jnp.transpose(
        contract("cs,ks->ck", payload, order_hot).reshape(4, -1, BLK), (1, 0, 2)
    )
    local_blocks = blocks.shape[0]
    seg_width = blocks.shape[2]
    flat_blocks = blocks.reshape(local_blocks, 4 * seg_width)
    source_local = pair_blocks[0]
    asked_hot = one_hot(asked, local_blocks)
    served = contract("pb,bw->pw", asked_hot, flat_blocks).reshape(devices, cap * 4 * seg_width)
    fetched = lax.all_to_all(served, ("px", "py"), 0, 0, tiled=True).reshape(
        devices * cap, 4 * seg_width
    )
    slot_hot = slot_match.astype(jnp.float32)
    source_hot = one_hot(source_local, local_blocks)
    target_rows = contract("ps,sw->pw", slot_hot, fetched).reshape(pairs, 4, seg_width)
    source_rows = contract("pb,bw->pw", source_hot, flat_blocks).reshape(pairs, 4, seg_width)
    on_target, on_source = evaluate(target_rows, source_rows)
    returned = contract("ps,pw->sw", slot_hot, on_target)
    arrived = lax.all_to_all(
        returned.reshape(devices, cap * seg_width), ("px", "py"), 0, 0, tiled=True
    ).reshape(devices * cap, seg_width)
    block_force = contract("pb,pw->bw", asked_hot, arrived) + contract(
        "pb,pw->bw", source_hot, on_source
    )
    pair_force = contract("k,ks->s", block_force.reshape(-1), order_hot)
    rows = gamma.shape[0] * gamma.shape[1]
    row_hot = one_hot(cell_index // extent, rows)
    column_hot = one_hot(cell_index % extent, extent)
    picked = contract("sr,rc->sc", row_hot, stress.reshape(rows, extent))
    glide_force = weights * jnp.sum(picked * column_hot, axis=1) + pair_force
    update = (STEP_MOBILITY * weights * glide_force)[:, None] * column_hot
    new_gamma = (gamma.reshape(rows, extent) + contract("sr,sc->rc", row_hot, update)).reshape(
        gamma.shape
    )
    return (stress, glide_force, new_gamma)


def solution(mesh):
    in_specs = (
        P("px", "py", None),
        P(None, ("px", "py")),
        P(("px", "py")),
        P(("px", "py"), None),
        P(("px", "py")),
        P(("px", "py"), None),
        P(None, ("px", "py")),
    )
    out_specs = (P("px", "py", None), P(("px", "py")), P("px", "py", None))
    return jax.shard_map(shards, mesh=mesh, in_specs=in_specs, out_specs=out_specs, check_vma=False)
```

```python
import math

import jax
import jax.numpy as jnp
from jax import lax
from jax.experimental import pallas as pl
from jax.sharding import PartitionSpec as P

BLK = 128


POISSON = 0.34
STEP_MOBILITY = 0.5
CORE_SQUARED = 1.0
ROOT_HALF = 0.7071067811865476


def wrapped(indices, number):
    shifted = jnp.where(indices == number // 2, 0, indices - number)
    return jnp.where(indices < number // 2, indices, shifted).astype(jnp.float32)


def multiplier(first, second, third):
    summed = first * first + second * second + third * third
    bounded = jnp.maximum(summed, 1.0)
    normal_part = (first + second + third) ** 2 / (3.0 * bounded)
    slip_part = (first - second) ** 2 / (2.0 * bounded)
    factor = normal_part + slip_part - 2.0 * normal_part * slip_part / (1.0 - POISSON) - 1.0
    return jnp.where(summed > 0.5, factor, 0.0)


def pair_terms(target, source):
    offset = target[:, 0:3, :, None] - source[:, 0:3, None, :]
    squared = (
        offset[:, 0] * offset[:, 0]
        + offset[:, 1] * offset[:, 1]
        + offset[:, 2] * offset[:, 2]
        + CORE_SQUARED
    )
    along = (offset[:, 0] - offset[:, 1]) * ROOT_HALF
    strength = target[:, 3, :, None] * source[:, 3, None, :]
    coupling = strength * along / (squared * jnp.sqrt(squared))
    return (jnp.sum(coupling, axis=2), -jnp.sum(coupling, axis=1))


PAIR_STEP = 32


def pair_kernel(target_ref, source_ref, on_target_ref, on_source_ref):
    columns = jnp.transpose(target_ref[...].reshape(PAIR_STEP * 4, BLK))
    source_rows = []
    target_rows = []
    for p in range(PAIR_STEP):
        source = source_ref[p]
        d0 = columns[:, 4 * p : 4 * p + 1] - source[0:1, :]
        d1 = columns[:, 4 * p + 1 : 4 * p + 2] - source[1:2, :]
        d2 = columns[:, 4 * p + 2 : 4 * p + 3] - source[2:3, :]
        squared = d0 * d0 + d1 * d1 + d2 * d2 + CORE_SQUARED
        along = (d0 - d1) * ROOT_HALF
        strength = columns[:, 4 * p + 3 : 4 * p + 4] * source[3:4, :]
        root = lax.rsqrt(squared)
        coupling = strength * along * (root * root * root)
        source_rows.append(-jnp.sum(coupling, axis=0, keepdims=True))
        high = coupling.astype(jnp.bfloat16)
        low = (coupling - high.astype(jnp.float32)).astype(jnp.bfloat16)
        ones = jnp.ones((8, BLK), jnp.bfloat16)
        lanes = (((1,), (1,)), ((), ()))
        sums = lax.dot_general(
            ones, high, lanes, preferred_element_type=jnp.float32
        ) + lax.dot_general(ones, low, lanes, preferred_element_type=jnp.float32)
        target_rows.append(sums[0:1, :])
    on_source_ref[...] = jnp.concatenate(source_rows, 0)
    on_target_ref[...] = jnp.concatenate(target_rows, 0)


def evaluate(target, source):
    number = target.shape[0]
    width = target.shape[2]
    block_in = pl.BlockSpec((PAIR_STEP, 4, width), lambda i: (i, 0, 0))
    block_out = pl.BlockSpec((PAIR_STEP, width), lambda i: (i, 0))
    return pl.pallas_call(
        pair_kernel,
        grid=(number // PAIR_STEP,),
        in_specs=[block_in, block_in],
        out_specs=[block_out, block_out],
        out_shape=[jax.ShapeDtypeStruct((number, width), jnp.float32)] * 2,
    )(target, source)


def dft_tables(number):
    indices = jnp.arange(number, dtype=jnp.int32)
    phases = indices[:, None] * indices[None, :] % number
    angles = phases.astype(jnp.float32) * (2.0 * math.pi / number)
    return (jnp.cos(angles), jnp.sin(angles))


def contract(form, left, right):
    return jnp.einsum(form, left, right, precision=lax.Precision.HIGHEST)


def rotate(form, real_part, imag_part, cosines, sine_table, direction):
    real_out = contract(form, real_part, cosines) + direction * contract(
        form, imag_part, sine_table
    )
    imag_out = contract(form, imag_part, cosines) - direction * contract(
        form, real_part, sine_table
    )
    return (real_out, imag_out)


def across_rows(real_part, imag_part):
    return (
        lax.all_to_all(real_part, "py", split_axis=1, concat_axis=2, tiled=True),
        lax.all_to_all(imag_part, "py", split_axis=1, concat_axis=2, tiled=True),
    )


def across_columns(real_part, imag_part):
    return (
        lax.all_to_all(real_part, "px", split_axis=0, concat_axis=2, tiled=True),
        lax.all_to_all(imag_part, "px", split_axis=0, concat_axis=2, tiled=True),
    )


def cplx_table(number, direction):
    cosines, sine_table = dft_tables(number)
    top = jnp.stack([cosines, -direction * sine_table], 1)
    bottom = jnp.stack([direction * sine_table, cosines], 1)
    return jnp.stack([top, bottom], 0)


def one_hot(indices, number):
    return (indices[:, None] == jnp.arange(number, dtype=jnp.int32)[None, :]).astype(jnp.float32)


def shards(gamma, positions, weights, block_order, cell_index, pair_dest, pair_blocks):
    extent = gamma.shape[2]
    py_count = extent // gamma.shape[1]
    half = extent // 2 + 1
    kept = -(-half // py_count) * py_count
    cosines, sine_table = dft_tables(extent)
    live = (jnp.arange(kept) < half).astype(jnp.float32)
    cos_half = cosines[:, :kept] * live[None, :]
    sin_half = sine_table[:, :kept] * live[None, :]
    folds = jnp.where((jnp.arange(kept) == 0) | (jnp.arange(kept) == extent // 2), 1.0, 2.0) * live
    forward = cplx_table(extent, 1.0)
    inverse = cplx_table(extent, -1.0)
    destination = pair_dest[:, 0]
    target_block = pair_blocks[1]
    pairs = destination.shape[0]
    devices = lax.psum(1, ("px", "py"))
    px_count = devices // py_count
    cap = 2
    earlier = jnp.sum(
        (destination[:, None] == destination[None, :])
        & (jnp.arange(pairs)[:, None] > jnp.arange(pairs)[None, :]),
        axis=1,
        dtype=jnp.int32,
    )
    slot = destination * cap + earlier
    slot_match = slot[:, None] == jnp.arange(devices * cap, dtype=jnp.int32)[None, :]
    wanted = jnp.sum(jnp.where(slot_match, target_block[:, None], 0), axis=0, dtype=jnp.int32)
    wanted = wanted.astype(jnp.float32).reshape(px_count, py_count, cap)
    spec = contract("abx,xck->cakb", gamma, jnp.stack([cos_half, -sin_half], 1))
    c2, a2, k2, b2 = spec.shape
    sent = jnp.transpose(spec.reshape(c2, a2, py_count, k2 // py_count, b2), (2, 0, 1, 3, 4))
    sent = jnp.concatenate(
        [sent.reshape(py_count, -1), jnp.transpose(wanted, (1, 0, 2)).reshape(py_count, -1)], 1
    )
    got = lax.all_to_all(sent, "py", 0, 0, tiled=True)
    body = c2 * a2 * (k2 // py_count) * b2
    spec = jnp.transpose(
        got[:, :body].reshape(py_count, c2, a2, k2 // py_count, b2), (1, 2, 3, 0, 4)
    ).reshape(c2, a2, k2 // py_count, py_count * b2)
    relay = got[:, body:].reshape(py_count, px_count, cap)
    spec = contract("caky,cydm->dmka", spec, forward)
    c3, m3, k3, a3 = spec.shape
    sent = jnp.transpose(spec.reshape(c3, px_count, m3 // px_count, k3, a3), (1, 0, 2, 3, 4))
    sent = jnp.concatenate(
        [sent.reshape(px_count, -1), jnp.transpose(relay, (1, 0, 2)).reshape(px_count, -1)], 1
    )
    got = lax.all_to_all(sent, "px", 0, 0, tiled=True)
    body = c3 * (m3 // px_count) * k3 * a3
    spec = jnp.transpose(
        got[:, :body].reshape(px_count, c3, m3 // px_count, k3, a3), (1, 2, 3, 0, 4)
    ).reshape(c3, m3 // px_count, k3, px_count * a3)
    asked = got[:, body:].reshape(-1).astype(jnp.int32)
    spec = contract("cmkz,czdq->dmkq", spec, forward)
    rows_local = spec.shape[1]
    cols_local = spec.shape[2]
    first_index = lax.axis_index("px") * rows_local + jnp.arange(rows_local, dtype=jnp.int32)
    second_index = lax.axis_index("py") * cols_local + jnp.arange(cols_local, dtype=jnp.int32)
    third_index = jnp.arange(extent, dtype=jnp.int32)
    factor_table = multiplier(
        wrapped(third_index, extent)[None, None, :],
        wrapped(first_index, extent)[:, None, None],
        wrapped(second_index, extent)[None, :, None],
    )
    spec = spec * factor_table[None]
    seg_count = positions.shape[1]
    members = block_order[0]
    payload = jnp.concatenate([positions, weights[None, :]], 0)
    order_hot = one_hot(members, seg_count)
    blocks = jnp.transpose(
        contract("cs,ks->ck", payload, order_hot).reshape(4, -1, BLK), (1, 0, 2)
    )
    local_blocks = blocks.shape[0]
    seg_width = blocks.shape[2]
    flat_blocks = blocks.reshape(local_blocks, 4 * seg_width)
    source_local = pair_blocks[0]
    asked_hot = one_hot(asked, local_blocks)
    served = contract("pb,bw->pw", asked_hot, flat_blocks).reshape(devices, cap * 4 * seg_width)
    fetched = lax.all_to_all(served, ("px", "py"), 0, 0, tiled=True).reshape(
        devices * cap, 4 * seg_width
    )
    slot_hot = slot_match.astype(jnp.float32)
    source_hot = one_hot(source_local, local_blocks)
    target_rows = contract("ps,sw->pw", slot_hot, fetched).reshape(pairs, 4, seg_width)
    source_rows = contract("pb,bw->pw", source_hot, flat_blocks).reshape(pairs, 4, seg_width)
    on_target, on_source = evaluate(target_rows, source_rows)
    returned = contract("ps,pw->sw", slot_hot, on_target)
    forces = returned.reshape(px_count, py_count, cap * seg_width)
    spec = contract("cmkq,cqdz->dzkm", spec, inverse)
    c4, z4, k4, m4 = spec.shape
    sent = jnp.transpose(spec.reshape(c4, px_count, z4 // px_count, k4, m4), (1, 0, 2, 3, 4))
    sent = jnp.concatenate([sent.reshape(px_count, -1), forces.reshape(px_count, -1)], 1)
    got = lax.all_to_all(sent, "px", 0, 0, tiled=True)
    body = c4 * (z4 // px_count) * k4 * m4
    spec = jnp.transpose(
        got[:, :body].reshape(px_count, c4, z4 // px_count, k4, m4), (1, 2, 3, 0, 4)
    ).reshape(c4, z4 // px_count, k4, px_count * m4)
    relay = got[:, body:].reshape(px_count, py_count, cap * seg_width)
    spec = contract("cakm,cmdy->dayk", spec, inverse)
    c5, a5, y5, k5 = spec.shape
    sent = jnp.transpose(spec.reshape(c5, a5, py_count, y5 // py_count, k5), (2, 0, 1, 3, 4))
    sent = jnp.concatenate(
        [sent.reshape(py_count, -1), jnp.transpose(relay, (1, 0, 2)).reshape(py_count, -1)], 1
    )
    got = lax.all_to_all(sent, "py", 0, 0, tiled=True)
    body = c5 * a5 * (y5 // py_count) * k5
    spec = jnp.transpose(
        got[:, :body].reshape(py_count, c5, a5, y5 // py_count, k5), (1, 2, 3, 0, 4)
    ).reshape(c5, a5, y5 // py_count, py_count * k5)
    arrived = jnp.transpose(
        got[:, body:].reshape(py_count, px_count, cap, seg_width), (1, 0, 2, 3)
    ).reshape(devices * cap, seg_width)
    final_table = jnp.stack([folds[:, None] * cos_half.T, -folds[:, None] * sin_half.T], 0)
    stress = contract("cabk,ckx->abx", spec, final_table) / float(extent**3)
    block_force = contract("pb,pw->bw", asked_hot, arrived) + contract(
        "pb,pw->bw", source_hot, on_source
    )
    pair_force = contract("k,ks->s", block_force.reshape(-1), order_hot)
    rows = gamma.shape[0] * gamma.shape[1]
    row_hot = one_hot(cell_index // extent, rows)
    column_hot = one_hot(cell_index % extent, extent)
    picked = contract("sr,rc->sc", row_hot, stress.reshape(rows, extent))
    glide_force = weights * jnp.sum(picked * column_hot, axis=1) + pair_force
    update = (STEP_MOBILITY * weights * glide_force)[:, None] * column_hot
    new_gamma = (gamma.reshape(rows, extent) + contract("sr,sc->rc", row_hot, update)).reshape(
        gamma.shape
    )
    return (stress, glide_force, new_gamma)


def solution(mesh):
    in_specs = (
        P("px", "py", None),
        P(None, ("px", "py")),
        P(("px", "py")),
        P(("px", "py"), None),
        P(("px", "py")),
        P(("px", "py"), None),
        P(None, ("px", "py")),
    )
    out_specs = (P("px", "py", None), P(("px", "py")), P("px", "py", None))
    return jax.shard_map(shards, mesh=mesh, in_specs=in_specs, out_specs=out_specs, check_vma=False)
```
